128 devices in a mesh: src: 4 (over z), vol: 32 (over y, x, core).
Axes of the slice: x: 4, y: 4, z: 4, core: 2. Of those that a mesh axis runs over, the one named last changes fastest.
Arguments:
- forward: bfloat16 [16384, 36, 512], P(('src', 'vol')), may hold values from -6 to 6
- item_tx: int32 [16384], P(('src', 'vol')), may hold values from 0 to 15, as said below
- item_brick: int32 [16384], P(('src', 'vol')), may hold values from 0 to 1023
- tx_place: int32 [16], replicated, may hold values from 0 to 15, as said below
- brick_place: int32 [1024], replicated, may hold values from 0 to 1023, as said below
- adjoint: bfloat16 [16, 1024, 36, 512], P('src', 'vol'), may hold values from -6 to 6
Outputs:
- gradient: float32 [2, 256, 16, 128], P(None, 'vol')
The draws below stay inside these ranges and needn't reach their ends.
Inputs may be any that keep to these rules, and one draw needn't show every extreme that they name: Stored brick i goes to owner (tx_place[item_tx[i]] // 4, brick_place[item_brick[i]] // 32) as (src index, vol index). Among the stored bricks of one device at most 2 share an owner; in every draw one owner receives exactly 2 from every device. `tx_place`: A permutation. `brick_place`: A permutation.
All inputs are finite; a program needn't handle non-finite values.
Results may differ from the reference program's by a relative error of at most 0.0003.
Values may be sent and summed in bfloat16 or wider, within the bound.
No kernel may reach another device: no remote copies, remote signals or barrier semaphores. Data moves between devices by JAX's collectives and lax.ppermute only.
A program may use at most 128 MiB of HBM per device.

```python
import math
import jax
import jax.numpy as jnp
from jax import lax

E = 8
CELLS = 512
NFREQ = 6
CH = 36
NBY = 2
NBZ = 16
BR_OWN = 32
TX_DEV = 4
STORE = 128
CAP = 2
NTX = 16
NBRICKS = 1024
NX = 256
NY = 16
NZ = 128
N_VOL = 32
DEVICES = 128


def layout(key):
    base_key = jax.random.fold_in(key, 11)
    key_list = jax.random.split(base_key, 4)
    brick_place = jax.random.permutation(key_list[0], NBRICKS).astype(jnp.int32)
    tx_place = jax.random.permutation(key_list[1], NTX).astype(jnp.int32)
    brick_of = jnp.zeros((NBRICKS,), jnp.int32).at[brick_place].set(jnp.arange(NBRICKS, dtype=jnp.int32))
    tx_of = jnp.zeros((NTX,), jnp.int32).at[tx_place].set(jnp.arange(NTX, dtype=jnp.int32))
    hottest = jax.random.randint(key_list[2], (), 0, DEVICES).astype(jnp.int32)

    def one_device(device_key):
        sub_keys = jax.random.split(device_key, 4)
        spare_slots = jax.random.permutation(sub_keys[0], (DEVICES - 1) * CAP)[:STORE - CAP].astype(jnp.int32)
        others = spare_slots // CAP
        others = others + (others >= hottest).astype(jnp.int32)
        destination = jnp.concatenate([jnp.zeros((CAP,), jnp.int32) + hottest, others])
        local_tx = jax.random.randint(sub_keys[1], (STORE,), 0, TX_DEV).astype(jnp.int32)
        local_brick = jax.random.randint(sub_keys[2], (STORE,), 0, BR_OWN).astype(jnp.int32)
        tx_ids = tx_of[destination // N_VOL * TX_DEV + local_tx]
        brick_ids = brick_of[destination % N_VOL * BR_OWN + local_brick]
        shuffle = jax.random.permutation(sub_keys[3], STORE)
        return (tx_ids[shuffle], brick_ids[shuffle])
    tx_ids, brick_ids = jax.vmap(one_device)(jax.random.split(key_list[3], DEVICES))
    return (tx_ids.reshape(-1), brick_ids.reshape(-1), tx_place, brick_place)


def draw_item_tx(key, part):
    return layout(key)[0]


def draw_item_brick(key, part):
    return layout(key)[1]


def draw_tx_place(key, part):
    return layout(key)[2]


def draw_brick_place(key, part):
    return layout(key)[3]


def block_scale(stream_key, shape, shards, low, largest):
    gain = 1.0
    for axis_at, parts in shards:
        steps = jax.random.uniform(jax.random.fold_in(jax.random.fold_in(stream_key, 6), axis_at), (parts,), jnp.float32, low / len(shards), largest / len(shards))
        gain = gain * jnp.repeat(jnp.exp(steps), shape[axis_at] // parts).reshape((-1,) + (1,) * (len(shape) - 1 - axis_at))
    return gain


def noise(stream_key, shape, spread, reach, cuts=(), kind=jnp.bfloat16):
    loudness = block_scale(stream_key, shape, cuts, -0.22, 0.18) if cuts else 1.0
    entries = jax.random.normal(stream_key, shape, jnp.float32) * spread * loudness
    return jnp.minimum(jnp.maximum(entries, -reach), reach).astype(kind)


def setup_inputs(seed: int = 0) -> dict:
    seeds = jax.random.split(jax.random.key(seed), 7)
    forward = noise(seeds[0], (DEVICES * STORE, CH, CELLS), 1.0, 6.0, ((0, 128),))
    item_tx = draw_item_tx(jax.random.fold_in(seeds[6], 71), 0)
    item_brick = draw_item_brick(jax.random.fold_in(seeds[6], 71), 0)
    tx_place = draw_tx_place(jax.random.fold_in(seeds[6], 71), 0)
    brick_place = draw_brick_place(jax.random.fold_in(seeds[6], 71), 0)
    adjoint = noise(seeds[5], (NTX, NBRICKS, CH, CELLS), 1.0, 6.0, ((0, 4), (1, 32)))
    return dict(forward=forward, item_tx=item_tx, item_brick=item_brick, tx_place=tx_place, brick_place=brick_place, adjoint=adjoint)


def tap_weights():
    raw_taps = [math.exp(-(offset - 4) * (offset - 4) / 4.5) for offset in range(9)]
    tap_total = sum(raw_taps)
    return [tap_value / tap_total for tap_value in raw_taps]


def correlate(fwd_field, adj_field):
    lead_shape = fwd_field.shape[:-2]
    fwd_split = fwd_field.reshape(lead_shape + (NFREQ, 3, 2, fwd_field.shape[-1]))
    adj_split = adj_field.reshape(lead_shape + (NFREQ, 3, 2, adj_field.shape[-1]))
    products = fwd_split[..., 0, :] * adj_split[..., 0, :] - fwd_split[..., 1, :] * adj_split[..., 1, :]
    horizontal = jnp.sum(products[..., 0:2, :], axis=(-3, -2))
    vertical = jnp.sum(products[..., 2, :], axis=-2)
    return jnp.stack([horizontal, vertical], axis=-2)


def smooth_axis(padded, axis):
    weights = tap_weights()
    length = padded.shape[axis] - 8
    summed = jnp.zeros(padded.shape[:axis] + (length,) + padded.shape[axis + 1:], jnp.float32)
    for offset in range(9):
        summed = summed + weights[offset] * lax.slice_in_dim(padded, offset, offset + length, axis=axis)
    return summed


def pad_axis(field, axis):
    widths = [(0, 0)] * field.ndim
    widths[axis] = (4, 4)
    return jnp.pad(field, widths)


def reference(forward, item_tx, item_brick, tx_place, brick_place, adjoint):
    tx_at = tx_place[item_tx].astype(jnp.int32)
    brick_at = brick_place[item_brick].astype(jnp.int32)
    fwd_blocks = forward.reshape(DEVICES, STORE, CH, CELLS)

    def step(gradient, block_items):
        fwd_part, tx_part, brick_part = block_items
        picked = adjoint[tx_part, brick_part]
        product = correlate(fwd_part.astype(jnp.float32), picked.astype(jnp.float32))
        return gradient.at[brick_part].add(product), None

    start = jnp.zeros((NBRICKS, 2, CELLS), jnp.float32)
    raw, _ = lax.scan(step, start, (fwd_blocks, tx_at.reshape(DEVICES, STORE), brick_at.reshape(DEVICES, STORE)))
    field = raw.reshape(N_VOL, NBY, NBZ, 2, E, E, E).transpose(3, 0, 4, 1, 5, 2, 6).reshape(2, NX, NY, NZ)
    for axis in (1, 2, 3):
        field = smooth_axis(pad_axis(field, axis), axis)
    return field
```

```python
import math

import jax
import jax.numpy as jnp
from jax import lax
from jax.experimental import pallas as pl
from jax.experimental.pallas import tpu as pltpu
from jax.sharding import PartitionSpec as P

E = 8
NFREQ = 6
NBY = 2
NBZ = 16
LANES = 128
META = 16


def with_halo(cells, sides, width):
    for axis, dim in sides:
        count = lax.axis_size(axis)
        ends = count - 1
        head = lax.slice_in_dim(cells, 0, width, axis=dim)
        tail = lax.slice_in_dim(cells, cells.shape[dim] - width, cells.shape[dim], axis=dim)
        cells = jnp.concatenate(
            [
                lax.ppermute(tail, axis, [(i, (i + 1) % count) for i in range(ends)]),
                cells,
                lax.ppermute(head, axis, [((i + 1) % count, i) for i in range(ends)]),
            ],
            axis=dim,
        )
    return cells


def tap_weights():
    raw_taps = [math.exp(-(offset - 4) * (offset - 4) / 4.5) for offset in range(9)]
    tap_total = sum(raw_taps)
    return [tap_value / tap_total for tap_value in raw_taps]


def smooth_axis(padded, axis):
    weights = tap_weights()
    length = padded.shape[axis] - 8
    summed = jnp.zeros(padded.shape[:axis] + (length,) + padded.shape[axis + 1 :], jnp.float32)
    for offset in range(9):
        summed = summed + weights[offset] * lax.slice_in_dim(
            padded, offset, offset + length, axis=axis
        )
    return summed


def pad_axis(field, axis):
    widths = [(0, 0)] * field.ndim
    widths[axis] = (4, 4)
    return jnp.pad(field, widths)


def lookup(indices, table):
    hits = indices[:, None] == jnp.arange(table.shape[0], dtype=jnp.int32)[None, :]
    return jnp.sum(jnp.where(hits, table[None, :], 0), axis=1)


def pack_kernel(src_ref, pair_ref, fwd_ref, out_ref):
    dests = out_ref.shape[0]
    rows = fwd_ref.shape[1]
    base = pl.program_id(0) * dests * 2

    def one_dest(d, carry):
        slot = base + 2 * d
        first = src_ref[slot]
        second = src_ref[slot + 1]
        out_ref[d, 0:rows, :] = fwd_ref[jnp.maximum(first, 0)]
        out_ref[d, rows : 2 * rows, :] = fwd_ref[jnp.maximum(second, 0)]
        row_at = lax.broadcasted_iota(jnp.int32, (META, LANES), 0)
        tags = jnp.where(row_at < META // 2, pair_ref[slot], pair_ref[slot + 1])
        out_ref[d, 2 * rows : 2 * rows + META, :] = tags.astype(jnp.float32).astype(out_ref.dtype)
        return carry

    lax.fori_loop(0, dests, one_dest, 0)


def correlate_kernel(pair_ref, arrived_ref, adj_ref, acc_ref):
    dests = arrived_ref.shape[0]
    rows = adj_ref.shape[2]
    bricks = adj_ref.shape[1]
    groups = rows // 8
    step = pl.program_id(0)

    @pl.when(step == 0)
    def _():
        acc_ref[...] = jnp.zeros(acc_ref.shape, acc_ref.dtype)

    base = step * dests * 2

    def one_slot(d, s):
        pair = pair_ref[base + 2 * d + s]

        @pl.when(pair >= 0)
        def _():
            tx = pair // bricks
            brick = pair % bricks
            fwd = arrived_ref[d, s * rows : (s + 1) * rows, :].astype(jnp.float32)
            adj = adj_ref[tx, brick].astype(jnp.float32)
            prod = (fwd * adj).reshape(groups, 8, LANES)
            horizontal = None
            vertical = None
            for g in range(groups):
                if g % 3 == 2:
                    vertical = prod[g] if vertical is None else vertical + prod[g]
                else:
                    horizontal = prod[g] if horizontal is None else horizontal + prod[g]
            acc_ref[brick, 0] += horizontal
            acc_ref[brick, 1] += vertical

    def one_dest(d, carry):
        one_slot(d, 0)
        one_slot(d, 1)
        return carry

    lax.fori_loop(0, dests, one_dest, 0)


def src_sum(part):
    count = lax.axis_size("src")
    me = lax.axis_index("src")
    parts = [part] + [
        lax.ppermute(part, "src", [(i, (i + k) % count) for i in range(count)])
        for k in range(1, count)
    ]
    stacked = jnp.stack(parts)
    total = lax.dynamic_index_in_dim(stacked, me % count, keepdims=False)
    for j in range(1, count):
        total = total + lax.dynamic_index_in_dim(stacked, (me - j) % count, keepdims=False)
    return total


def local(forward, item_tx, item_brick, tx_place, brick_place, adjoint):
    stored = forward.shape[0]
    channels = forward.shape[1]
    cells = forward.shape[2]
    rows = channels * cells // LANES
    src_count = lax.axis_size("src")
    vol_count = lax.axis_size("vol")
    devices = src_count * vol_count
    local_tx = adjoint.shape[0]
    local_bricks = adjoint.shape[1]
    capacity = 2
    slot_total = devices * capacity
    tx_at = lookup(item_tx, tx_place)
    brick_at = lookup(item_brick, brick_place)
    destination = tx_at // local_tx * vol_count + brick_at // local_bricks
    pair_index = tx_at % local_tx * local_bricks + brick_at % local_bricks
    positions = jnp.arange(stored, dtype=jnp.int32)
    same_owner = destination[:, None] == destination[None, :]
    earlier = positions[:, None] > positions[None, :]
    order_rank = jnp.sum((same_owner & earlier).astype(jnp.int32), axis=1)
    slot_index = destination * capacity + order_rank
    slot_hits = slot_index[None, :] == jnp.arange(slot_total, dtype=jnp.int32)[:, None]
    filled = jnp.any(slot_hits, axis=1)
    src_of_slot = jnp.where(
        filled, jnp.sum(jnp.where(slot_hits, positions[None, :], 0), axis=1), -1
    ).astype(jnp.int32)
    pair_of_slot = jnp.where(
        filled, jnp.sum(jnp.where(slot_hits, pair_index[None, :], 0), axis=1), -1
    ).astype(jnp.int32)

    fwd_rows = forward.reshape(stored, rows, LANES)
    chunk = 2 * rows + META
    pack_steps = 8
    dests_per_step = devices // pack_steps
    payload = pl.pallas_call(
        pack_kernel,
        out_shape=jax.ShapeDtypeStruct((devices, chunk, LANES), forward.dtype),
        grid_spec=pltpu.PrefetchScalarGridSpec(
            num_scalar_prefetch=2,
            grid=(pack_steps,),
            in_specs=[pl.BlockSpec((stored, rows, LANES), lambda g, s, p: (0, 0, 0))],
            out_specs=pl.BlockSpec((dests_per_step, chunk, LANES), lambda g, s, p: (g, 0, 0)),
        ),
        compiler_params=pltpu.CompilerParams(vmem_limit_bytes=48 * 1024 * 1024),
    )(src_of_slot, pair_of_slot, fwd_rows)

    arrived = lax.all_to_all(payload, ("src", "vol"), split_axis=0, concat_axis=0, tiled=True)
    tags = jnp.stack(
        [arrived[:, 2 * rows, 0], arrived[:, 2 * rows + META // 2, 0]], axis=1
    ).reshape(slot_total)
    arrived_pairs = tags.astype(jnp.float32).astype(jnp.int32)

    adj_rows = adjoint.reshape(local_tx, local_bricks, rows, LANES)
    acc = pl.pallas_call(
        correlate_kernel,
        out_shape=jax.ShapeDtypeStruct((local_bricks, 2, 8, LANES), jnp.float32),
        grid_spec=pltpu.PrefetchScalarGridSpec(
            num_scalar_prefetch=1,
            grid=(pack_steps,),
            in_specs=[
                pl.BlockSpec((dests_per_step, chunk, LANES), lambda g, p: (g, 0, 0)),
                pl.BlockSpec((local_tx, local_bricks, rows, LANES), lambda g, p: (0, 0, 0, 0)),
            ],
            out_specs=pl.BlockSpec((local_bricks, 2, 8, LANES), lambda g, p: (0, 0, 0, 0)),
        ),
        compiler_params=pltpu.CompilerParams(vmem_limit_bytes=48 * 1024 * 1024),
    )(arrived_pairs, arrived, adj_rows)

    gradient = (acc[:, :, 0:4, :] - acc[:, :, 4:8, :]).reshape(local_bricks, 2, cells)
    slab = (
        gradient.reshape(NBY, NBZ, 2, E, E, E)
        .transpose(2, 3, 0, 4, 1, 5)
        .reshape(2, E, NBY * E, NBZ * E)
    )
    summed = src_sum(slab)
    padded = with_halo(summed, (("vol", 1),), 4)
    field = smooth_axis(padded, 1)
    for axis in (2, 3):
        field = smooth_axis(pad_axis(field, axis), axis)
    return field


def solution(mesh):
    in_specs = (
        P(("src", "vol"), None, None),
        P(("src", "vol")),
        P(("src", "vol")),
        P(),
        P(),
        P("src", "vol", None, None),
    )
    out_specs = P(None, "vol", None, None)
    return jax.shard_map(local, mesh=mesh, in_specs=in_specs, out_specs=out_specs, check_vma=False)
```

```python
import math

import jax
import jax.numpy as jnp
from jax import lax
from jax.experimental import pallas as pl
from jax.experimental.pallas import tpu as pltpu
from jax.sharding import PartitionSpec as P

E = 8
NFREQ = 6
NBY = 2
NBZ = 16
LANES = 128
META = 16


def tap_weights():
    raw_taps = [math.exp(-(offset - 4) * (offset - 4) / 4.5) for offset in range(9)]
    tap_total = sum(raw_taps)
    return [tap_value / tap_total for tap_value in raw_taps]


def smooth_axis(padded, axis):
    weights = tap_weights()
    length = padded.shape[axis] - 8
    summed = jnp.zeros(padded.shape[:axis] + (length,) + padded.shape[axis + 1 :], jnp.float32)
    for offset in range(9):
        summed = summed + weights[offset] * lax.slice_in_dim(
            padded, offset, offset + length, axis=axis
        )
    return summed


def pad_axis(field, axis):
    widths = [(0, 0)] * field.ndim
    widths[axis] = (4, 4)
    return jnp.pad(field, widths)


def lookup(indices, table):
    hits = indices[:, None] == jnp.arange(table.shape[0], dtype=jnp.int32)[None, :]
    return jnp.sum(jnp.where(hits, table[None, :], 0), axis=1)


def pack_kernel(src_ref, pair_ref, fwd_ref, out_ref):
    dests = out_ref.shape[0]
    rows = fwd_ref.shape[1]
    base = pl.program_id(0) * dests * 2

    def one_dest(d, carry):
        slot = base + 2 * d
        first = src_ref[slot]
        second = src_ref[slot + 1]
        out_ref[d, 0:rows, :] = fwd_ref[jnp.maximum(first, 0)]
        out_ref[d, rows : 2 * rows, :] = fwd_ref[jnp.maximum(second, 0)]
        row_at = lax.broadcasted_iota(jnp.int32, (META, LANES), 0)
        tags = jnp.where(row_at < META // 2, pair_ref[slot], pair_ref[slot + 1])
        out_ref[d, 2 * rows : 2 * rows + META, :] = tags.astype(jnp.float32).astype(out_ref.dtype)
        return carry

    lax.fori_loop(0, dests, one_dest, 0)


def correlate_kernel(pair_ref, arrived_ref, adj_ref, acc_ref):
    dests = arrived_ref.shape[0]
    rows = adj_ref.shape[2]
    bricks = adj_ref.shape[1]
    groups = rows // 8
    step = pl.program_id(0)

    @pl.when(step == 0)
    def _():
        acc_ref[...] = jnp.zeros(acc_ref.shape, acc_ref.dtype)

    base = step * dests * 2

    def one_slot(d, s):
        pair = pair_ref[base + 2 * d + s]

        @pl.when(pair >= 0)
        def _():
            tx = pair // bricks
            brick = pair % bricks
            fwd = arrived_ref[d, s * rows : (s + 1) * rows, :].astype(jnp.float32)
            adj = adj_ref[tx, brick].astype(jnp.float32)
            prod = (fwd * adj).reshape(groups, 8, LANES)
            horizontal = None
            vertical = None
            for g in range(groups):
                if g % 3 == 2:
                    vertical = prod[g] if vertical is None else vertical + prod[g]
                else:
                    horizontal = prod[g] if horizontal is None else horizontal + prod[g]
            acc_ref[brick, 0] += horizontal
            acc_ref[brick, 1] += vertical

    def one_dest(d, carry):
        one_slot(d, 0)
        one_slot(d, 1)
        return carry

    lax.fori_loop(0, dests, one_dest, 0, unroll=4)


def canonical_sum(received, me, count):
    stacked = jnp.stack(received)
    total = lax.dynamic_index_in_dim(stacked, me % count, keepdims=False)
    for j in range(1, count):
        total = total + lax.dynamic_index_in_dim(stacked, (me - j) % count, keepdims=False)
    return total


def summed_with_halo(part, width):
    src_count = lax.axis_size("src")
    vol_count = lax.axis_size("vol")
    me = lax.axis_index("src")
    axes = ("src", "vol")

    def flat(s, v):
        return s * vol_count + v

    head = part[:, :width]
    tail = part[:, part.shape[1] - width :]
    centre = [part]
    from_left = []
    from_right = []
    for k in range(src_count):
        if k:
            centre.append(
                lax.ppermute(
                    part,
                    axes,
                    [(flat(s, v), flat((s + k) % src_count, v)) for s in range(src_count) for v in range(vol_count)],
                )
            )
        from_left.append(
            lax.ppermute(
                tail,
                axes,
                [
                    (flat(s, v), flat((s + k) % src_count, v + 1))
                    for s in range(src_count)
                    for v in range(vol_count - 1)
                ],
            )
        )
        from_right.append(
            lax.ppermute(
                head,
                axes,
                [
                    (flat(s, v + 1), flat((s + k) % src_count, v))
                    for s in range(src_count)
                    for v in range(vol_count - 1)
                ],
            )
        )
    summed = canonical_sum(centre, me, src_count)
    left = canonical_sum(from_left, me, src_count)
    right = canonical_sum(from_right, me, src_count)
    return jnp.concatenate([left, summed, right], axis=1)


def local(forward, item_tx, item_brick, tx_place, brick_place, adjoint):
    stored = forward.shape[0]
    channels = forward.shape[1]
    cells = forward.shape[2]
    rows = channels * cells // LANES
    src_count = lax.axis_size("src")
    vol_count = lax.axis_size("vol")
    devices = src_count * vol_count
    local_tx = adjoint.shape[0]
    local_bricks = adjoint.shape[1]
    capacity = 2
    slot_total = devices * capacity
    tx_at = lookup(item_tx, tx_place)
    brick_at = lookup(item_brick, brick_place)
    destination = tx_at // local_tx * vol_count + brick_at // local_bricks
    pair_index = tx_at % local_tx * local_bricks + brick_at % local_bricks
    positions = jnp.arange(stored, dtype=jnp.int32)
    same_owner = destination[:, None] == destination[None, :]
    earlier = positions[:, None] > positions[None, :]
    order_rank = jnp.sum((same_owner & earlier).astype(jnp.int32), axis=1)
    slot_index = destination * capacity + order_rank
    slot_hits = slot_index[None, :] == jnp.arange(slot_total, dtype=jnp.int32)[:, None]
    filled = jnp.any(slot_hits, axis=1)
    src_of_slot = jnp.where(
        filled, jnp.sum(jnp.where(slot_hits, positions[None, :], 0), axis=1), -1
    ).astype(jnp.int32)
    pair_of_slot = jnp.where(
        filled, jnp.sum(jnp.where(slot_hits, pair_index[None, :], 0), axis=1), -1
    ).astype(jnp.int32)

    fwd_rows = forward.reshape(stored, rows, LANES)
    chunk = 2 * rows + META
    pack_steps = 8
    dests_per_step = devices // pack_steps
    payload = pl.pallas_call(
        pack_kernel,
        out_shape=jax.ShapeDtypeStruct((devices, chunk, LANES), forward.dtype),
        grid_spec=pltpu.PrefetchScalarGridSpec(
            num_scalar_prefetch=2,
            grid=(pack_steps,),
            in_specs=[pl.BlockSpec((stored, rows, LANES), lambda g, s, p: (0, 0, 0))],
            out_specs=pl.BlockSpec((dests_per_step, chunk, LANES), lambda g, s, p: (g, 0, 0)),
        ),
        compiler_params=pltpu.CompilerParams(vmem_limit_bytes=48 * 1024 * 1024),
    )(src_of_slot, pair_of_slot, fwd_rows)

    arrived = lax.all_to_all(payload, ("src", "vol"), split_axis=0, concat_axis=0, tiled=True)
    tags = jnp.stack(
        [arrived[:, 2 * rows, 0], arrived[:, 2 * rows + META // 2, 0]], axis=1
    ).reshape(slot_total)
    arrived_pairs = tags.astype(jnp.float32).astype(jnp.int32)

    adj_rows = adjoint.reshape(local_tx, local_bricks, rows, LANES)
    acc = pl.pallas_call(
        correlate_kernel,
        out_shape=jax.ShapeDtypeStruct((local_bricks, 2, 8, LANES), jnp.float32),
        grid_spec=pltpu.PrefetchScalarGridSpec(
            num_scalar_prefetch=1,
            grid=(pack_steps,),
            in_specs=[
                pl.BlockSpec((dests_per_step, chunk, LANES), lambda g, p: (g, 0, 0)),
                pl.BlockSpec((local_tx, local_bricks, rows, LANES), lambda g, p: (0, 0, 0, 0)),
            ],
            out_specs=pl.BlockSpec((local_bricks, 2, 8, LANES), lambda g, p: (0, 0, 0, 0)),
        ),
        compiler_params=pltpu.CompilerParams(vmem_limit_bytes=48 * 1024 * 1024),
    )(arrived_pairs, arrived, adj_rows)

    gradient = (acc[:, :, 0:4, :] - acc[:, :, 4:8, :]).reshape(local_bricks, 2, cells)
    slab = (
        gradient.reshape(NBY, NBZ, 2, E, E, E)
        .transpose(2, 3, 0, 4, 1, 5)
        .reshape(2, E, NBY * E, NBZ * E)
    )
    padded = summed_with_halo(slab, 4)
    field = smooth_axis(padded, 1)
    for axis in (2, 3):
        field = smooth_axis(pad_axis(field, axis), axis)
    return field


def solution(mesh):
    in_specs = (
        P(("src", "vol"), None, None),
        P(("src", "vol")),
        P(("src", "vol")),
        P(),
        P(),
        P("src", "vol", None, None),
    )
    out_specs = P(None, "vol", None, None)
    return jax.shard_map(local, mesh=mesh, in_specs=in_specs, out_specs=out_specs, check_vma=False)
```

```python
import math

import jax
import jax.numpy as jnp
from jax import lax
from jax.experimental import pallas as pl
from jax.experimental.pallas import tpu as pltpu
from jax.sharding import PartitionSpec as P

E = 8
NFREQ = 6
NBY = 2
NBZ = 16
LANES = 128
META = 16


def with_halo(cells, sides, width):
    for axis, dim in sides:
        count = lax.axis_size(axis)
        ends = count - 1
        head = lax.slice_in_dim(cells, 0, width, axis=dim)
        tail = lax.slice_in_dim(cells, cells.shape[dim] - width, cells.shape[dim], axis=dim)
        cells = jnp.concatenate(
            [
                lax.ppermute(tail, axis, [(i, (i + 1) % count) for i in range(ends)]),
                cells,
                lax.ppermute(head, axis, [((i + 1) % count, i) for i in range(ends)]),
            ],
            axis=dim,
        )
    return cells


def tap_weights():
    raw_taps = [math.exp(-(offset - 4) * (offset - 4) / 4.5) for offset in range(9)]
    tap_total = sum(raw_taps)
    return [tap_value / tap_total for tap_value in raw_taps]


def smooth_axis(padded, axis):
    weights = tap_weights()
    length = padded.shape[axis] - 8
    summed = jnp.zeros(padded.shape[:axis] + (length,) + padded.shape[axis + 1 :], jnp.float32)
    for offset in range(9):
        summed = summed + weights[offset] * lax.slice_in_dim(
            padded, offset, offset + length, axis=axis
        )
    return summed


def pad_axis(field, axis):
    widths = [(0, 0)] * field.ndim
    widths[axis] = (4, 4)
    return jnp.pad(field, widths)


def lookup(indices, table):
    hits = indices[:, None] == jnp.arange(table.shape[0], dtype=jnp.int32)[None, :]
    return jnp.sum(jnp.where(hits, table[None, :], 0), axis=1)


def pack_kernel(src_ref, pair_ref, fwd_ref, out_ref):
    dests = out_ref.shape[0]
    rows = fwd_ref.shape[1]
    base = pl.program_id(0) * dests * 2

    def one_dest(d, carry):
        slot = base + 2 * d
        first = src_ref[slot]
        second = src_ref[slot + 1]
        out_ref[d, 0:rows, :] = fwd_ref[jnp.maximum(first, 0)]
        out_ref[d, rows : 2 * rows, :] = fwd_ref[jnp.maximum(second, 0)]
        row_at = lax.broadcasted_iota(jnp.int32, (META, LANES), 0)
        tags = jnp.where(row_at < META // 2, pair_ref[slot], pair_ref[slot + 1])
        out_ref[d, 2 * rows : 2 * rows + META, :] = tags.astype(jnp.float32).astype(out_ref.dtype)
        return carry

    lax.fori_loop(0, dests, one_dest, 0)


def correlate_kernel(pair_ref, arrived_ref, adj_ref, acc_ref):
    dests = arrived_ref.shape[0]
    rows = adj_ref.shape[2]
    bricks = adj_ref.shape[1]
    groups = rows // 8
    step = pl.program_id(0)

    @pl.when(step == 0)
    def _():
        acc_ref[...] = jnp.zeros(acc_ref.shape, acc_ref.dtype)

    base = step * dests * 2

    def one_slot(d, s):
        pair = pair_ref[base + 2 * d + s]

        @pl.when(pair >= 0)
        def _():
            tx = pair // bricks
            brick = pair % bricks
            fwd = arrived_ref[d, s * rows : (s + 1) * rows, :].astype(jnp.float32)
            adj = adj_ref[tx, brick].astype(jnp.float32)
            prod = (fwd * adj).reshape(groups, 8, LANES)
            horizontal = None
            vertical = None
            for g in range(groups):
                if g % 3 == 2:
                    vertical = prod[g] if vertical is None else vertical + prod[g]
                else:
                    horizontal = prod[g] if horizontal is None else horizontal + prod[g]
            acc_ref[brick, 0] += horizontal
            acc_ref[brick, 1] += vertical

    def one_dest(d, carry):
        one_slot(d, 0)
        one_slot(d, 1)
        return carry

    lax.fori_loop(0, dests, one_dest, 0)


def src_sum(part):
    count = lax.axis_size("src")
    me = lax.axis_index("src")
    parts = [part] + [
        lax.ppermute(part, "src", [(i, (i + k) % count) for i in range(count)])
        for k in range(1, count)
    ]
    stacked = jnp.stack(parts)
    total = lax.dynamic_index_in_dim(stacked, me % count, keepdims=False)
    for j in range(1, count):
        total = total + lax.dynamic_index_in_dim(stacked, (me - j) % count, keepdims=False)
    return total


def local(forward, item_tx, item_brick, tx_place, brick_place, adjoint):
    stored = forward.shape[0]
    channels = forward.shape[1]
    cells = forward.shape[2]
    rows = channels * cells // LANES
    src_count = lax.axis_size("src")
    vol_count = lax.axis_size("vol")
    devices = src_count * vol_count
    local_tx = adjoint.shape[0]
    local_bricks = adjoint.shape[1]
    capacity = 2
    slot_total = devices * capacity
    tx_at = lookup(item_tx, tx_place)
    brick_at = lookup(item_brick, brick_place)
    destination = tx_at // local_tx * vol_count + brick_at // local_bricks
    pair_index = tx_at % local_tx * local_bricks + brick_at % local_bricks
    positions = jnp.arange(stored, dtype=jnp.int32)
    same_owner = destination[:, None] == destination[None, :]
    earlier = positions[:, None] > positions[None, :]
    order_rank = jnp.sum((same_owner & earlier).astype(jnp.int32), axis=1)
    slot_index = destination * capacity + order_rank
    slot_hits = slot_index[None, :] == jnp.arange(slot_total, dtype=jnp.int32)[:, None]
    filled = jnp.any(slot_hits, axis=1)
    src_of_slot = jnp.where(
        filled, jnp.sum(jnp.where(slot_hits, positions[None, :], 0), axis=1), -1
    ).astype(jnp.int32)
    pair_of_slot = jnp.where(
        filled, jnp.sum(jnp.where(slot_hits, pair_index[None, :], 0), axis=1), -1
    ).astype(jnp.int32)

    fwd_rows = jnp.transpose(
        jnp.transpose(forward, (1, 0, 2)).reshape(channels, stored, cells // LANES, LANES), (1, 0, 2, 3)
    ).reshape(stored, rows, LANES)
    chunk = 2 * rows + META
    pack_steps = 8
    dests_per_step = devices // pack_steps
    payload = pl.pallas_call(
        pack_kernel,
        out_shape=jax.ShapeDtypeStruct((devices, chunk, LANES), forward.dtype),
        grid_spec=pltpu.PrefetchScalarGridSpec(
            num_scalar_prefetch=2,
            grid=(pack_steps,),
            in_specs=[pl.BlockSpec((stored, rows, LANES), lambda g, s, p: (0, 0, 0))],
            out_specs=pl.BlockSpec((dests_per_step, chunk, LANES), lambda g, s, p: (g, 0, 0)),
        ),
        compiler_params=pltpu.CompilerParams(vmem_limit_bytes=48 * 1024 * 1024),
    )(src_of_slot, pair_of_slot, fwd_rows)

    arrived = lax.all_to_all(payload, ("src", "vol"), split_axis=0, concat_axis=0, tiled=True)
    tags = jnp.stack(
        [arrived[:, 2 * rows, 0], arrived[:, 2 * rows + META // 2, 0]], axis=1
    ).reshape(slot_total)
    arrived_pairs = tags.astype(jnp.float32).astype(jnp.int32)

    adj_rows = jnp.transpose(
        jnp.transpose(adjoint, (0, 2, 1, 3)).reshape(local_tx, channels, local_bricks, cells // LANES, LANES),
        (0, 2, 1, 3, 4),
    ).reshape(local_tx, local_bricks, rows, LANES)
    acc = pl.pallas_call(
        correlate_kernel,
        out_shape=jax.ShapeDtypeStruct((local_bricks, 2, 8, LANES), jnp.float32),
        grid_spec=pltpu.PrefetchScalarGridSpec(
            num_scalar_prefetch=1,
            grid=(pack_steps,),
            in_specs=[
                pl.BlockSpec((dests_per_step, chunk, LANES), lambda g, p: (g, 0, 0)),
                pl.BlockSpec((local_tx, local_bricks, rows, LANES), lambda g, p: (0, 0, 0, 0)),
            ],
            out_specs=pl.BlockSpec((local_bricks, 2, 8, LANES), lambda g, p: (0, 0, 0, 0)),
        ),
        compiler_params=pltpu.CompilerParams(vmem_limit_bytes=48 * 1024 * 1024),
    )(arrived_pairs, arrived, adj_rows)

    gradient = (acc[:, :, 0:4, :] - acc[:, :, 4:8, :]).reshape(local_bricks, 2, cells)
    slab = (
        gradient.reshape(NBY, NBZ, 2, E, E, E)
        .transpose(2, 3, 0, 4, 1, 5)
        .reshape(2, E, NBY * E, NBZ * E)
    )
    summed = src_sum(slab)
    padded = with_halo(summed, (("vol", 1),), 4)
    field = smooth_axis(padded, 1)
    for axis in (2, 3):
        field = smooth_axis(pad_axis(field, axis), axis)
    return field


def solution(mesh):
    in_specs = (
        P(("src", "vol"), None, None),
        P(("src", "vol")),
        P(("src", "vol")),
        P(),
        P(),
        P("src", "vol", None, None),
    )
    out_specs = P(None, "vol", None, None)
    return jax.shard_map(local, mesh=mesh, in_specs=in_specs, out_specs=out_specs, check_vma=False)
```

```python
import math

import jax
import jax.numpy as jnp
from jax import lax
from jax.experimental import pallas as pl
from jax.experimental.pallas import tpu as pltpu
from jax.sharding import PartitionSpec as P

E = 8
NFREQ = 6
NBY = 2
NBZ = 16
LANES = 128
META = 16


def with_halo(cells, sides, width):
    for axis, dim in sides:
        count = lax.axis_size(axis)
        ends = count - 1
        head = lax.slice_in_dim(cells, 0, width, axis=dim)
        tail = lax.slice_in_dim(cells, cells.shape[dim] - width, cells.shape[dim], axis=dim)
        cells = jnp.concatenate(
            [
                lax.ppermute(tail, axis, [(i, (i + 1) % count) for i in range(ends)]),
                cells,
                lax.ppermute(head, axis, [((i + 1) % count, i) for i in range(ends)]),
            ],
            axis=dim,
        )
    return cells


def tap_weights():
    raw_taps = [math.exp(-(offset - 4) * (offset - 4) / 4.5) for offset in range(9)]
    tap_total = sum(raw_taps)
    return [tap_value / tap_total for tap_value in raw_taps]


def smooth_axis(padded, axis):
    weights = tap_weights()
    length = padded.shape[axis] - 8
    summed = jnp.zeros(padded.shape[:axis] + (length,) + padded.shape[axis + 1 :], jnp.float32)
    for offset in range(9):
        summed = summed + weights[offset] * lax.slice_in_dim(
            padded, offset, offset + length, axis=axis
        )
    return summed


def pad_axis(field, axis):
    widths = [(0, 0)] * field.ndim
    widths[axis] = (4, 4)
    return jnp.pad(field, widths)


def lookup(indices, table):
    hits = indices[:, None] == jnp.arange(table.shape[0], dtype=jnp.int32)[None, :]
    return jnp.sum(jnp.where(hits, table[None, :], 0), axis=1)


def pack_kernel(src_ref, pair_ref, fwd_ref, out_ref):
    dests = out_ref.shape[0]
    rows = fwd_ref.shape[1]
    base = pl.program_id(0) * dests * 2

    def one_dest(d, carry):
        slot = base + 2 * d
        first = src_ref[slot]
        second = src_ref[slot + 1]
        out_ref[d, 0:rows, :] = fwd_ref[jnp.maximum(first, 0)]
        out_ref[d, rows : 2 * rows, :] = fwd_ref[jnp.maximum(second, 0)]
        row_at = lax.broadcasted_iota(jnp.int32, (META, LANES), 0)
        tags = jnp.where(row_at < META // 2, pair_ref[slot], pair_ref[slot + 1])
        out_ref[d, 2 * rows : 2 * rows + META, :] = tags.astype(jnp.float32).astype(out_ref.dtype)
        return carry

    lax.fori_loop(0, dests, one_dest, 0)


def correlate_kernel(pair_ref, arrived_ref, adj_ref, out_ref):
    dests = arrived_ref.shape[0]
    rows = adj_ref.shape[2]
    bricks = adj_ref.shape[1]
    groups = rows // 8
    base = pl.program_id(0) * dests * 2

    def one_slot(d, s):
        k = 2 * d + s
        pair = pair_ref[base + k]
        held = jnp.maximum(pair, 0)
        fwd = arrived_ref[d, s * rows : (s + 1) * rows, :].astype(jnp.float32)
        adj = adj_ref[held // bricks, held % bricks].astype(jnp.float32)
        prod = (fwd * adj).reshape(groups, 8, LANES)
        horizontal = None
        vertical = None
        for g in range(groups):
            if g % 3 == 2:
                vertical = prod[g] if vertical is None else vertical + prod[g]
            else:
                horizontal = prod[g] if horizontal is None else horizontal + prod[g]
        out_ref[k, 0] = jnp.where(pair >= 0, horizontal, 0.0)
        out_ref[k, 1] = jnp.where(pair >= 0, vertical, 0.0)

    for d in range(dests):
        one_slot(d, 0)
        one_slot(d, 1)


def src_sum(part):
    count = lax.axis_size("src")
    me = lax.axis_index("src")
    parts = [part] + [
        lax.ppermute(part, "src", [(i, (i + k) % count) for i in range(count)])
        for k in range(1, count)
    ]
    stacked = jnp.stack(parts)
    total = lax.dynamic_index_in_dim(stacked, me % count, keepdims=False)
    for j in range(1, count):
        total = total + lax.dynamic_index_in_dim(stacked, (me - j) % count, keepdims=False)
    return total


def local(forward, item_tx, item_brick, tx_place, brick_place, adjoint):
    stored = forward.shape[0]
    channels = forward.shape[1]
    cells = forward.shape[2]
    rows = channels * cells // LANES
    src_count = lax.axis_size("src")
    vol_count = lax.axis_size("vol")
    devices = src_count * vol_count
    local_tx = adjoint.shape[0]
    local_bricks = adjoint.shape[1]
    capacity = 2
    slot_total = devices * capacity
    tx_at = lookup(item_tx, tx_place)
    brick_at = lookup(item_brick, brick_place)
    destination = tx_at // local_tx * vol_count + brick_at // local_bricks
    pair_index = tx_at % local_tx * local_bricks + brick_at % local_bricks
    positions = jnp.arange(stored, dtype=jnp.int32)
    same_owner = destination[:, None] == destination[None, :]
    earlier = positions[:, None] > positions[None, :]
    order_rank = jnp.sum((same_owner & earlier).astype(jnp.int32), axis=1)
    slot_index = destination * capacity + order_rank
    slot_hits = slot_index[None, :] == jnp.arange(slot_total, dtype=jnp.int32)[:, None]
    filled = jnp.any(slot_hits, axis=1)
    src_of_slot = jnp.where(
        filled, jnp.sum(jnp.where(slot_hits, positions[None, :], 0), axis=1), -1
    ).astype(jnp.int32)
    pair_of_slot = jnp.where(
        filled, jnp.sum(jnp.where(slot_hits, pair_index[None, :], 0), axis=1), -1
    ).astype(jnp.int32)

    fwd_rows = jnp.transpose(
        jnp.transpose(forward, (1, 0, 2)).reshape(channels, stored, cells // LANES, LANES), (1, 0, 2, 3)
    ).reshape(stored, rows, LANES)
    chunk = 2 * rows + META
    pack_steps = 8
    dests_per_step = devices // pack_steps
    payload = pl.pallas_call(
        pack_kernel,
        out_shape=jax.ShapeDtypeStruct((devices, chunk, LANES), forward.dtype),
        grid_spec=pltpu.PrefetchScalarGridSpec(
            num_scalar_prefetch=2,
            grid=(pack_steps,),
            in_specs=[pl.BlockSpec((stored, rows, LANES), lambda g, s, p: (0, 0, 0))],
            out_specs=pl.BlockSpec((dests_per_step, chunk, LANES), lambda g, s, p: (g, 0, 0)),
        ),
        compiler_params=pltpu.CompilerParams(vmem_limit_bytes=48 * 1024 * 1024),
    )(src_of_slot, pair_of_slot, fwd_rows)

    arrived = lax.all_to_all(payload, ("src", "vol"), split_axis=0, concat_axis=0, tiled=True)
    tags = jnp.stack(
        [arrived[:, 2 * rows, 0], arrived[:, 2 * rows + META // 2, 0]], axis=1
    ).reshape(slot_total)
    arrived_pairs = tags.astype(jnp.float32).astype(jnp.int32)

    adj_rows = jnp.transpose(
        jnp.transpose(adjoint, (0, 2, 1, 3)).reshape(local_tx, channels, local_bricks, cells // LANES, LANES),
        (0, 2, 1, 3, 4),
    ).reshape(local_tx, local_bricks, rows, LANES)
    per_slot = pl.pallas_call(
        correlate_kernel,
        out_shape=jax.ShapeDtypeStruct((slot_total, 2, 8, LANES), jnp.float32),
        grid_spec=pltpu.PrefetchScalarGridSpec(
            num_scalar_prefetch=1,
            grid=(pack_steps,),
            in_specs=[
                pl.BlockSpec((dests_per_step, chunk, LANES), lambda g, p: (g, 0, 0)),
                pl.BlockSpec((local_tx, local_bricks, rows, LANES), lambda g, p: (0, 0, 0, 0)),
            ],
            out_specs=pl.BlockSpec((2 * dests_per_step, 2, 8, LANES), lambda g, p: (g, 0, 0, 0)),
        ),
        compiler_params=pltpu.CompilerParams(vmem_limit_bytes=48 * 1024 * 1024),
    )(arrived_pairs, arrived, adj_rows)

    corr = (per_slot[:, :, 0:4, :] - per_slot[:, :, 4:8, :]).reshape(slot_total, 2 * cells)
    owner_brick = jnp.maximum(arrived_pairs, 0) % local_bricks
    owner_table = (
        (owner_brick[None, :] == jnp.arange(local_bricks, dtype=jnp.int32)[:, None])
        & (arrived_pairs >= 0)[None, :]
    ).astype(jnp.float32)
    gradient = jnp.dot(owner_table, corr, precision=lax.Precision.HIGHEST).reshape(local_bricks, 2, cells)
    slab = (
        gradient.reshape(NBY, NBZ, 2, E, E, E)
        .transpose(2, 3, 0, 4, 1, 5)
        .reshape(2, E, NBY * E, NBZ * E)
    )
    summed = src_sum(slab)
    padded = with_halo(summed, (("vol", 1),), 4)
    field = smooth_axis(padded, 1)
    for axis in (2, 3):
        field = smooth_axis(pad_axis(field, axis), axis)
    return field


def solution(mesh):
    in_specs = (
        P(("src", "vol"), None, None),
        P(("src", "vol")),
        P(("src", "vol")),
        P(),
        P(),
        P("src", "vol", None, None),
    )
    out_specs = P(None, "vol", None, None)
    return jax.shard_map(local, mesh=mesh, in_specs=in_specs, out_specs=out_specs, check_vma=False)
```

```python
import math

import jax
import jax.numpy as jnp
from jax import lax
from jax.experimental import pallas as pl
from jax.experimental.pallas import tpu as pltpu
from jax.sharding import PartitionSpec as P

E = 8
NFREQ = 6
NBY = 2
NBZ = 16
LANES = 128
META = 16


def with_halo(cells, sides, width):
    for axis, dim in sides:
        count = lax.axis_size(axis)
        ends = count - 1
        head = lax.slice_in_dim(cells, 0, width, axis=dim)
        tail = lax.slice_in_dim(cells, cells.shape[dim] - width, cells.shape[dim], axis=dim)
        cells = jnp.concatenate(
            [
                lax.ppermute(tail, axis, [(i, (i + 1) % count) for i in range(ends)]),
                cells,
                lax.ppermute(head, axis, [((i + 1) % count, i) for i in range(ends)]),
            ],
            axis=dim,
        )
    return cells


def tap_weights():
    raw_taps = [math.exp(-(offset - 4) * (offset - 4) / 4.5) for offset in range(9)]
    tap_total = sum(raw_taps)
    return [tap_value / tap_total for tap_value in raw_taps]


def smooth_axis(padded, axis):
    weights = tap_weights()
    length = padded.shape[axis] - 8
    summed = jnp.zeros(padded.shape[:axis] + (length,) + padded.shape[axis + 1 :], jnp.float32)
    for offset in range(9):
        summed = summed + weights[offset] * lax.slice_in_dim(
            padded, offset, offset + length, axis=axis
        )
    return summed


def pad_axis(field, axis):
    widths = [(0, 0)] * field.ndim
    widths[axis] = (4, 4)
    return jnp.pad(field, widths)


def lookup(indices, table):
    hits = indices[:, None] == jnp.arange(table.shape[0], dtype=jnp.int32)[None, :]
    return jnp.sum(jnp.where(hits, table[None, :], 0), axis=1)


def pack_kernel(src_ref, pair_ref, fwd_ref, out_ref):
    dests = out_ref.shape[0]
    rows = fwd_ref.shape[1]
    base = pl.program_id(0) * dests * 2

    def one_dest(d, carry):
        slot = base + 2 * d
        first = src_ref[slot]
        second = src_ref[slot + 1]
        out_ref[d, 0:rows, :] = fwd_ref[jnp.maximum(first, 0)]
        out_ref[d, rows : 2 * rows, :] = fwd_ref[jnp.maximum(second, 0)]
        row_at = lax.broadcasted_iota(jnp.int32, (META, LANES), 0)
        tags = jnp.where(row_at < META // 2, pair_ref[slot], pair_ref[slot + 1])
        out_ref[d, 2 * rows : 2 * rows + META, :] = tags.astype(jnp.float32).astype(out_ref.dtype)
        return carry

    lax.fori_loop(0, dests, one_dest, 0)


def correlate_kernel(pair_ref, arrived_hbm, adj_hbm, out_ref, fwd_buf, adj_buf, fwd_sem, adj_sem):
    slots = out_ref.shape[0]
    rows = adj_buf.shape[2]
    bricks = adj_buf.shape[1]
    groups = rows // 8
    adj_copy = pltpu.make_async_copy(adj_hbm, adj_buf, adj_sem.at[0])
    adj_copy.start()

    def slot_copy(k):
        return pltpu.make_async_copy(
            arrived_hbm.at[k // 2, pl.ds((k % 2) * rows, rows)], fwd_buf.at[k], fwd_sem.at[k]
        )

    def start(k, carry):
        @pl.when(pair_ref[k] >= 0)
        def _():
            slot_copy(k).start()

        return carry

    lax.fori_loop(0, slots, start, 0)
    adj_copy.wait()

    def one_slot(k, carry):
        pair = pair_ref[k]

        @pl.when(pair >= 0)
        def _():
            slot_copy(k).wait()
            fwd = fwd_buf[k].astype(jnp.float32)
            adj = adj_buf[pair // bricks, pair % bricks].astype(jnp.float32)
            prod = (fwd * adj).reshape(groups, 8, LANES)
            horizontal = None
            vertical = None
            for g in range(groups):
                if g % 3 == 2:
                    vertical = prod[g] if vertical is None else vertical + prod[g]
                else:
                    horizontal = prod[g] if horizontal is None else horizontal + prod[g]
            out_ref[k, 0] = horizontal
            out_ref[k, 1] = vertical

        @pl.when(pair < 0)
        def _():
            out_ref[k] = jnp.zeros(out_ref.shape[1:], out_ref.dtype)

        return carry

    lax.fori_loop(0, slots, one_slot, 0)


def src_sum(part):
    count = lax.axis_size("src")
    me = lax.axis_index("src")
    parts = [part] + [
        lax.ppermute(part, "src", [(i, (i + k) % count) for i in range(count)])
        for k in range(1, count)
    ]
    stacked = jnp.stack(parts)
    total = lax.dynamic_index_in_dim(stacked, me % count, keepdims=False)
    for j in range(1, count):
        total = total + lax.dynamic_index_in_dim(stacked, (me - j) % count, keepdims=False)
    return total


def local(forward, item_tx, item_brick, tx_place, brick_place, adjoint):
    stored = forward.shape[0]
    channels = forward.shape[1]
    cells = forward.shape[2]
    rows = channels * cells // LANES
    src_count = lax.axis_size("src")
    vol_count = lax.axis_size("vol")
    devices = src_count * vol_count
    local_tx = adjoint.shape[0]
    local_bricks = adjoint.shape[1]
    capacity = 2
    slot_total = devices * capacity
    tx_at = lookup(item_tx, tx_place)
    brick_at = lookup(item_brick, brick_place)
    destination = tx_at // local_tx * vol_count + brick_at // local_bricks
    pair_index = tx_at % local_tx * local_bricks + brick_at % local_bricks
    positions = jnp.arange(stored, dtype=jnp.int32)
    same_owner = destination[:, None] == destination[None, :]
    earlier = positions[:, None] > positions[None, :]
    order_rank = jnp.sum((same_owner & earlier).astype(jnp.int32), axis=1)
    slot_index = destination * capacity + order_rank
    slot_hits = slot_index[None, :] == jnp.arange(slot_total, dtype=jnp.int32)[:, None]
    filled = jnp.any(slot_hits, axis=1)
    src_of_slot = jnp.where(
        filled, jnp.sum(jnp.where(slot_hits, positions[None, :], 0), axis=1), -1
    ).astype(jnp.int32)
    pair_of_slot = jnp.where(
        filled, jnp.sum(jnp.where(slot_hits, pair_index[None, :], 0), axis=1), -1
    ).astype(jnp.int32)

    fwd_rows = jnp.transpose(
        jnp.transpose(forward, (1, 0, 2)).reshape(channels, stored, cells // LANES, LANES), (1, 0, 2, 3)
    ).reshape(stored, rows, LANES)
    chunk = 2 * rows + META
    pack_steps = 8
    dests_per_step = devices // pack_steps
    payload = pl.pallas_call(
        pack_kernel,
        out_shape=jax.ShapeDtypeStruct((devices, chunk, LANES), forward.dtype),
        grid_spec=pltpu.PrefetchScalarGridSpec(
            num_scalar_prefetch=2,
            grid=(pack_steps,),
            in_specs=[pl.BlockSpec((stored, rows, LANES), lambda g, s, p: (0, 0, 0))],
            out_specs=pl.BlockSpec((dests_per_step, chunk, LANES), lambda g, s, p: (g, 0, 0)),
        ),
        compiler_params=pltpu.CompilerParams(vmem_limit_bytes=48 * 1024 * 1024),
    )(src_of_slot, pair_of_slot, fwd_rows)

    arrived = lax.all_to_all(payload, ("src", "vol"), split_axis=0, concat_axis=0, tiled=True)
    tags = jnp.stack(
        [arrived[:, 2 * rows, 0], arrived[:, 2 * rows + META // 2, 0]], axis=1
    ).reshape(slot_total)
    arrived_pairs = tags.astype(jnp.float32).astype(jnp.int32)

    adj_rows = jnp.transpose(
        jnp.transpose(adjoint, (0, 2, 1, 3)).reshape(local_tx, channels, local_bricks, cells // LANES, LANES),
        (0, 2, 1, 3, 4),
    ).reshape(local_tx, local_bricks, rows, LANES)
    per_slot = pl.pallas_call(
        correlate_kernel,
        out_shape=jax.ShapeDtypeStruct((slot_total, 2, 8, LANES), jnp.float32),
        grid_spec=pltpu.PrefetchScalarGridSpec(
            num_scalar_prefetch=1,
            grid=(),
            in_specs=[pl.BlockSpec(memory_space=pl.ANY), pl.BlockSpec(memory_space=pl.ANY)],
            out_specs=pl.BlockSpec(memory_space=pltpu.VMEM),
            scratch_shapes=[
                pltpu.VMEM((slot_total, rows, LANES), forward.dtype),
                pltpu.VMEM(adj_rows.shape, adj_rows.dtype),
                pltpu.SemaphoreType.DMA((slot_total,)),
                pltpu.SemaphoreType.DMA((1,)),
            ],
        ),
        compiler_params=pltpu.CompilerParams(vmem_limit_bytes=48 * 1024 * 1024),
    )(arrived_pairs, arrived, adj_rows)

    corr = (per_slot[:, :, 0:4, :] - per_slot[:, :, 4:8, :]).reshape(slot_total, 2 * cells)
    owner_brick = jnp.maximum(arrived_pairs, 0) % local_bricks
    owner_table = (
        (owner_brick[None, :] == jnp.arange(local_bricks, dtype=jnp.int32)[:, None])
        & (arrived_pairs >= 0)[None, :]
    ).astype(jnp.float32)
    gradient = jnp.dot(owner_table, corr, precision=lax.Precision.HIGHEST).reshape(local_bricks, 2, cells)
    slab = (
        gradient.reshape(NBY, NBZ, 2, E, E, E)
        .transpose(2, 3, 0, 4, 1, 5)
        .reshape(2, E, NBY * E, NBZ * E)
    )
    summed = src_sum(slab)
    padded = with_halo(summed, (("vol", 1),), 4)
    field = smooth_axis(padded, 1)
    for axis in (2, 3):
        field = smooth_axis(pad_axis(field, axis), axis)
    return field


def solution(mesh):
    in_specs = (
        P(("src", "vol"), None, None),
        P(("src", "vol")),
        P(("src", "vol")),
        P(),
        P(),
        P("src", "vol", None, None),
    )
    out_specs = P(None, "vol", None, None)
    return jax.shard_map(local, mesh=mesh, in_specs=in_specs, out_specs=out_specs, check_vma=False)
```

```python
import math

import jax
import jax.numpy as jnp
from jax import lax
from jax.experimental import pallas as pl
from jax.experimental.pallas import tpu as pltpu
from jax.sharding import PartitionSpec as P

E = 8
NFREQ = 6
NBY = 2
NBZ = 16
LANES = 128
META = 16


def with_halo(cells, sides, width):
    for axis, dim in sides:
        count = lax.axis_size(axis)
        ends = count - 1
        head = lax.slice_in_dim(cells, 0, width, axis=dim)
        tail = lax.slice_in_dim(cells, cells.shape[dim] - width, cells.shape[dim], axis=dim)
        cells = jnp.concatenate(
            [
                lax.ppermute(tail, axis, [(i, (i + 1) % count) for i in range(ends)]),
                cells,
                lax.ppermute(head, axis, [((i + 1) % count, i) for i in range(ends)]),
            ],
            axis=dim,
        )
    return cells


def tap_weights():
    raw_taps = [math.exp(-(offset - 4) * (offset - 4) / 4.5) for offset in range(9)]
    tap_total = sum(raw_taps)
    return [tap_value / tap_total for tap_value in raw_taps]


def smooth_axis(padded, axis):
    weights = tap_weights()
    length = padded.shape[axis] - 8
    summed = jnp.zeros(padded.shape[:axis] + (length,) + padded.shape[axis + 1 :], jnp.float32)
    for offset in range(9):
        summed = summed + weights[offset] * lax.slice_in_dim(
            padded, offset, offset + length, axis=axis
        )
    return summed


def pad_axis(field, axis):
    widths = [(0, 0)] * field.ndim
    widths[axis] = (4, 4)
    return jnp.pad(field, widths)


def lookup(indices, table):
    hits = indices[:, None] == jnp.arange(table.shape[0], dtype=jnp.int32)[None, :]
    return jnp.sum(jnp.where(hits, table[None, :], 0), axis=1)


def pack_kernel(src_ref, pair_ref, fwd_ref, out_ref):
    dests = out_ref.shape[0]
    rows = fwd_ref.shape[1]
    base = pl.program_id(0) * dests * 2

    def one_dest(d, carry):
        slot = base + 2 * d
        first = src_ref[slot]
        second = src_ref[slot + 1]
        out_ref[d, 0:rows, :] = fwd_ref[jnp.maximum(first, 0)]
        out_ref[d, rows : 2 * rows, :] = fwd_ref[jnp.maximum(second, 0)]
        lane_at = lax.broadcasted_iota(jnp.int32, (META, LANES), 1)
        tags = jnp.where(lane_at == 0, pair_ref[slot], pair_ref[slot + 1])
        out_ref[d, 2 * rows : 2 * rows + META, :] = tags.astype(jnp.float32).astype(out_ref.dtype)
        return carry

    lax.fori_loop(0, dests, one_dest, 0)


def correlate_kernel(pair_ref, arrived_ref, adj_ref, out_ref):
    dests = arrived_ref.shape[0]
    rows = adj_ref.shape[2]
    bricks = adj_ref.shape[1]
    groups = rows // 8
    base = pl.program_id(0) * dests * 2

    def one_slot(d, s):
        k = 2 * d + s
        pair = pair_ref[base + k]
        held = jnp.maximum(pair, 0)
        fwd = arrived_ref[d, s * rows : (s + 1) * rows, :].astype(jnp.float32)
        adj = adj_ref[held // bricks, held % bricks].astype(jnp.float32)
        prod = (fwd * adj).reshape(groups, 8, LANES)
        horizontal = None
        vertical = None
        for g in range(groups):
            if g % 3 == 2:
                vertical = prod[g] if vertical is None else vertical + prod[g]
            else:
                horizontal = prod[g] if horizontal is None else horizontal + prod[g]
        out_ref[k, 0] = jnp.where(pair >= 0, horizontal, 0.0)
        out_ref[k, 1] = jnp.where(pair >= 0, vertical, 0.0)

    for d in range(dests):
        one_slot(d, 0)
        one_slot(d, 1)


def src_sum(part):
    count = lax.axis_size("src")
    me = lax.axis_index("src")
    parts = [part] + [
        lax.ppermute(part, "src", [(i, (i + k) % count) for i in range(count)])
        for k in range(1, count)
    ]
    stacked = jnp.stack(parts)
    total = lax.dynamic_index_in_dim(stacked, me % count, keepdims=False)
    for j in range(1, count):
        total = total + lax.dynamic_index_in_dim(stacked, (me - j) % count, keepdims=False)
    return total


def local(forward, item_tx, item_brick, tx_place, brick_place, adjoint):
    stored = forward.shape[0]
    channels = forward.shape[1]
    cells = forward.shape[2]
    rows = channels * cells // LANES
    src_count = lax.axis_size("src")
    vol_count = lax.axis_size("vol")
    devices = src_count * vol_count
    local_tx = adjoint.shape[0]
    local_bricks = adjoint.shape[1]
    capacity = 2
    slot_total = devices * capacity
    tx_at = lookup(item_tx, tx_place)
    brick_at = lookup(item_brick, brick_place)
    destination = tx_at // local_tx * vol_count + brick_at // local_bricks
    pair_index = tx_at % local_tx * local_bricks + brick_at % local_bricks
    positions = jnp.arange(stored, dtype=jnp.int32)
    same_owner = destination[:, None] == destination[None, :]
    earlier = positions[:, None] > positions[None, :]
    order_rank = jnp.sum((same_owner & earlier).astype(jnp.int32), axis=1)
    slot_index = destination * capacity + order_rank
    slot_hits = slot_index[None, :] == jnp.arange(slot_total, dtype=jnp.int32)[:, None]
    filled = jnp.any(slot_hits, axis=1)
    src_of_slot = jnp.where(
        filled, jnp.sum(jnp.where(slot_hits, positions[None, :], 0), axis=1), -1
    ).astype(jnp.int32)
    pair_of_slot = jnp.where(
        filled, jnp.sum(jnp.where(slot_hits, pair_index[None, :], 0), axis=1), -1
    ).astype(jnp.int32)

    fwd_rows = jnp.transpose(
        jnp.transpose(forward, (1, 0, 2)).reshape(channels, stored, cells // LANES, LANES), (1, 0, 2, 3)
    ).reshape(stored, rows, LANES)
    chunk = 2 * rows + META
    pack_steps = 8
    correlate_steps = 4
    dests_per_step = devices // pack_steps
    payload = pl.pallas_call(
        pack_kernel,
        out_shape=jax.ShapeDtypeStruct((devices, chunk, LANES), forward.dtype),
        grid_spec=pltpu.PrefetchScalarGridSpec(
            num_scalar_prefetch=2,
            grid=(pack_steps,),
            in_specs=[pl.BlockSpec((stored, rows, LANES), lambda g, s, p: (0, 0, 0))],
            out_specs=pl.BlockSpec((dests_per_step, chunk, LANES), lambda g, s, p: (g, 0, 0)),
        ),
        compiler_params=pltpu.CompilerParams(vmem_limit_bytes=48 * 1024 * 1024),
    )(src_of_slot, pair_of_slot, fwd_rows)

    arrived = lax.all_to_all(payload, ("src", "vol"), split_axis=0, concat_axis=0, tiled=True)
    tags = arrived[:, 2 * rows, 0:2].reshape(slot_total)
    arrived_pairs = tags.astype(jnp.float32).astype(jnp.int32)

    adj_rows = jnp.transpose(
        jnp.transpose(adjoint, (0, 2, 1, 3)).reshape(local_tx, channels, local_bricks, cells // LANES, LANES),
        (0, 2, 1, 3, 4),
    ).reshape(local_tx, local_bricks, rows, LANES)
    per_slot = pl.pallas_call(
        correlate_kernel,
        out_shape=jax.ShapeDtypeStruct((slot_total, 2, 8, LANES), jnp.float32),
        grid_spec=pltpu.PrefetchScalarGridSpec(
            num_scalar_prefetch=1,
            grid=(correlate_steps,),
            in_specs=[
                pl.BlockSpec((devices // correlate_steps, chunk, LANES), lambda g, p: (g, 0, 0)),
                pl.BlockSpec((local_tx, local_bricks, rows, LANES), lambda g, p: (0, 0, 0, 0)),
            ],
            out_specs=pl.BlockSpec((2 * devices // correlate_steps, 2, 8, LANES), lambda g, p: (g, 0, 0, 0)),
        ),
        compiler_params=pltpu.CompilerParams(vmem_limit_bytes=48 * 1024 * 1024),
    )(arrived_pairs, arrived, adj_rows)

    corr = (per_slot[:, :, 0:4, :] - per_slot[:, :, 4:8, :]).reshape(slot_total, 2 * cells)
    owner_brick = jnp.maximum(arrived_pairs, 0) % local_bricks
    owner_table = (
        (owner_brick[None, :] == jnp.arange(local_bricks, dtype=jnp.int32)[:, None])
        & (arrived_pairs >= 0)[None, :]
    ).astype(jnp.float32)
    gradient = jnp.dot(owner_table, corr, precision=lax.Precision.HIGHEST).reshape(local_bricks, 2, cells)
    slab = (
        gradient.reshape(NBY, NBZ, 2, E, E, E)
        .transpose(2, 3, 0, 4, 1, 5)
        .reshape(2, E, NBY * E, NBZ * E)
    )
    summed = src_sum(slab)
    padded = with_halo(summed, (("vol", 1),), 4)
    field = smooth_axis(padded, 1)
    for axis in (2, 3):
        field = smooth_axis(pad_axis(field, axis), axis)
    return field


def solution(mesh):
    in_specs = (
        P(("src", "vol"), None, None),
        P(("src", "vol")),
        P(("src", "vol")),
        P(),
        P(),
        P("src", "vol", None, None),
    )
    out_specs = P(None, "vol", None, None)
    return jax.shard_map(local, mesh=mesh, in_specs=in_specs, out_specs=out_specs, check_vma=False)
```

```python
import math

import jax
import jax.numpy as jnp
from jax import lax
from jax.experimental import pallas as pl
from jax.experimental.pallas import tpu as pltpu
from jax.sharding import PartitionSpec as P

E = 8
NFREQ = 6
NBY = 2
NBZ = 16
LANES = 128
META = 16


def with_halo(cells, sides, width):
    for axis, dim in sides:
        count = lax.axis_size(axis)
        ends = count - 1
        head = lax.slice_in_dim(cells, 0, width, axis=dim)
        tail = lax.slice_in_dim(cells, cells.shape[dim] - width, cells.shape[dim], axis=dim)
        cells = jnp.concatenate(
            [
                lax.ppermute(tail, axis, [(i, (i + 1) % count) for i in range(ends)]),
                cells,
                lax.ppermute(head, axis, [((i + 1) % count, i) for i in range(ends)]),
            ],
            axis=dim,
        )
    return cells


def tap_weights():
    raw_taps = [math.exp(-(offset - 4) * (offset - 4) / 4.5) for offset in range(9)]
    tap_total = sum(raw_taps)
    return [tap_value / tap_total for tap_value in raw_taps]


def smooth_axis(padded, axis):
    weights = tap_weights()
    length = padded.shape[axis] - 8
    summed = jnp.zeros(padded.shape[:axis] + (length,) + padded.shape[axis + 1 :], jnp.float32)
    for offset in range(9):
        summed = summed + weights[offset] * lax.slice_in_dim(
            padded, offset, offset + length, axis=axis
        )
    return summed


def pad_axis(field, axis):
    widths = [(0, 0)] * field.ndim
    widths[axis] = (4, 4)
    return jnp.pad(field, widths)


def lookup(indices, table):
    hits = indices[:, None] == jnp.arange(table.shape[0], dtype=jnp.int32)[None, :]
    return jnp.sum(jnp.where(hits, table[None, :], 0), axis=1)


def pack_kernel(src_ref, pair_ref, fwd_ref, out_ref):
    dests = out_ref.shape[0]
    rows = fwd_ref.shape[1]
    base = pl.program_id(0) * dests * 2

    def one_dest(d, carry):
        slot = base + 2 * d
        first = src_ref[slot]
        second = src_ref[slot + 1]
        out_ref[d, 0:rows, :] = fwd_ref[jnp.maximum(first, 0)]
        out_ref[d, rows : 2 * rows, :] = fwd_ref[jnp.maximum(second, 0)]
        lane_at = lax.broadcasted_iota(jnp.int32, (META, LANES), 1)
        tags = jnp.where(lane_at == 0, pair_ref[slot], pair_ref[slot + 1])
        out_ref[d, 2 * rows : 2 * rows + META, :] = tags.astype(jnp.float32).astype(out_ref.dtype)
        return carry

    lax.fori_loop(0, dests, one_dest, 0)


def correlate_kernel(pair_ref, arrived_ref, adj_ref, out_ref):
    dests = arrived_ref.shape[0]
    rows = adj_ref.shape[2]
    bricks = adj_ref.shape[1]
    groups = rows // 8
    base = pl.program_id(0) * dests * 2

    def one_slot(d, s):
        k = 2 * d + s
        pair = pair_ref[base + k]
        held = jnp.maximum(pair, 0)
        fwd = arrived_ref[d, s * rows : (s + 1) * rows, :].astype(jnp.float32)
        adj = adj_ref[held // bricks, held % bricks].astype(jnp.float32)
        prod = (fwd * adj).reshape(groups, 8, LANES)
        horizontal = None
        vertical = None
        for g in range(groups):
            if g % 3 == 2:
                vertical = prod[g] if vertical is None else vertical + prod[g]
            else:
                horizontal = prod[g] if horizontal is None else horizontal + prod[g]
        out_ref[k, 0] = jnp.where(pair >= 0, horizontal, 0.0)
        out_ref[k, 1] = jnp.where(pair >= 0, vertical, 0.0)

    for d in range(dests):
        one_slot(d, 0)
        one_slot(d, 1)


def src_sum(part):
    count = lax.axis_size("src")
    me = lax.axis_index("src")
    parts = [part] + [
        lax.ppermute(part, "src", [(i, (i + k) % count) for i in range(count)])
        for k in range(1, count)
    ]
    stacked = jnp.stack(parts)
    total = lax.dynamic_index_in_dim(stacked, me % count, keepdims=False)
    for j in range(1, count):
        total = total + lax.dynamic_index_in_dim(stacked, (me - j) % count, keepdims=False)
    return total


def local(forward, item_tx, item_brick, tx_place, brick_place, adjoint):
    stored = forward.shape[0]
    channels = forward.shape[1]
    cells = forward.shape[2]
    rows = channels * cells // LANES
    src_count = lax.axis_size("src")
    vol_count = lax.axis_size("vol")
    devices = src_count * vol_count
    local_tx = adjoint.shape[0]
    local_bricks = adjoint.shape[1]
    capacity = 2
    slot_total = devices * capacity
    tx_at = lookup(item_tx, tx_place)
    brick_at = lookup(item_brick, brick_place)
    destination = tx_at // local_tx * vol_count + brick_at // local_bricks
    pair_index = tx_at % local_tx * local_bricks + brick_at % local_bricks
    positions = jnp.arange(stored, dtype=jnp.int32)
    same_owner = destination[:, None] == destination[None, :]
    earlier = positions[:, None] > positions[None, :]
    order_rank = jnp.sum((same_owner & earlier).astype(jnp.int32), axis=1)
    slot_index = destination * capacity + order_rank
    slot_hits = slot_index[None, :] == jnp.arange(slot_total, dtype=jnp.int32)[:, None]
    filled = jnp.any(slot_hits, axis=1)
    src_of_slot = jnp.where(
        filled, jnp.sum(jnp.where(slot_hits, positions[None, :], 0), axis=1), -1
    ).astype(jnp.int32)
    pair_of_slot = jnp.where(
        filled, jnp.sum(jnp.where(slot_hits, pair_index[None, :], 0), axis=1), -1
    ).astype(jnp.int32)

    fwd_rows = jnp.transpose(
        jnp.transpose(forward, (1, 0, 2)).reshape(channels, stored, cells // LANES, LANES), (1, 0, 2, 3)
    ).reshape(stored, rows, LANES)
    chunk = 2 * rows + META
    pack_steps = 8
    correlate_steps = 2
    dests_per_step = devices // pack_steps
    payload = pl.pallas_call(
        pack_kernel,
        out_shape=jax.ShapeDtypeStruct((devices, chunk, LANES), forward.dtype),
        grid_spec=pltpu.PrefetchScalarGridSpec(
            num_scalar_prefetch=2,
            grid=(pack_steps,),
            in_specs=[pl.BlockSpec((stored, rows, LANES), lambda g, s, p: (0, 0, 0))],
            out_specs=pl.BlockSpec((dests_per_step, chunk, LANES), lambda g, s, p: (g, 0, 0)),
        ),
        compiler_params=pltpu.CompilerParams(vmem_limit_bytes=48 * 1024 * 1024),
    )(src_of_slot, pair_of_slot, fwd_rows)

    arrived = lax.all_to_all(payload, ("src", "vol"), split_axis=0, concat_axis=0, tiled=True)
    tags = arrived[:, 2 * rows, 0:2].reshape(slot_total)
    arrived_pairs = tags.astype(jnp.float32).astype(jnp.int32)

    adj_rows = jnp.transpose(
        jnp.transpose(adjoint, (0, 2, 1, 3)).reshape(local_tx, channels, local_bricks, cells // LANES, LANES),
        (0, 2, 1, 3, 4),
    ).reshape(local_tx, local_bricks, rows, LANES)
    per_slot = pl.pallas_call(
        correlate_kernel,
        out_shape=jax.ShapeDtypeStruct((slot_total, 2, 8, LANES), jnp.float32),
        grid_spec=pltpu.PrefetchScalarGridSpec(
            num_scalar_prefetch=1,
            grid=(correlate_steps,),
            in_specs=[
                pl.BlockSpec((devices // correlate_steps, chunk, LANES), lambda g, p: (g, 0, 0)),
                pl.BlockSpec((local_tx, local_bricks, rows, LANES), lambda g, p: (0, 0, 0, 0)),
            ],
            out_specs=pl.BlockSpec((2 * devices // correlate_steps, 2, 8, LANES), lambda g, p: (g, 0, 0, 0)),
        ),
        compiler_params=pltpu.CompilerParams(vmem_limit_bytes=48 * 1024 * 1024),
    )(arrived_pairs, arrived, adj_rows)

    corr = (per_slot[:, :, 0:4, :] - per_slot[:, :, 4:8, :]).reshape(slot_total, 2 * cells)
    owner_brick = jnp.maximum(arrived_pairs, 0) % local_bricks
    owner_table = (
        (owner_brick[None, :] == jnp.arange(local_bricks, dtype=jnp.int32)[:, None])
        & (arrived_pairs >= 0)[None, :]
    ).astype(jnp.float32)
    gradient = jnp.dot(owner_table, corr, precision=lax.Precision.HIGHEST).reshape(local_bricks, 2, cells)
    slab = (
        gradient.reshape(NBY, NBZ, 2, E, E, E)
        .transpose(2, 3, 0, 4, 1, 5)
        .reshape(2, E, NBY * E, NBZ * E)
    )
    summed = src_sum(slab)
    padded = with_halo(summed, (("vol", 1),), 4)
    field = smooth_axis(padded, 1)
    for axis in (2, 3):
        field = smooth_axis(pad_axis(field, axis), axis)
    return field


def solution(mesh):
    in_specs = (
        P(("src", "vol"), None, None),
        P(("src", "vol")),
        P(("src", "vol")),
        P(),
        P(),
        P("src", "vol", None, None),
    )
    out_specs = P(None, "vol", None, None)
    return jax.shard_map(local, mesh=mesh, in_specs=in_specs, out_specs=out_specs, check_vma=False)
```

```python
import math

import jax
import jax.numpy as jnp
from jax import lax
from jax.experimental import pallas as pl
from jax.experimental.pallas import tpu as pltpu
from jax.sharding import PartitionSpec as P

E = 8
NFREQ = 6
NBY = 2
NBZ = 16
LANES = 128
META = 16


def with_halo(cells, sides, width):
    for axis, dim in sides:
        count = lax.axis_size(axis)
        ends = count - 1
        head = lax.slice_in_dim(cells, 0, width, axis=dim)
        tail = lax.slice_in_dim(cells, cells.shape[dim] - width, cells.shape[dim], axis=dim)
        cells = jnp.concatenate(
            [
                lax.ppermute(tail, axis, [(i, (i + 1) % count) for i in range(ends)]),
                cells,
                lax.ppermute(head, axis, [((i + 1) % count, i) for i in range(ends)]),
            ],
            axis=dim,
        )
    return cells


def tap_weights():
    raw_taps = [math.exp(-(offset - 4) * (offset - 4) / 4.5) for offset in range(9)]
    tap_total = sum(raw_taps)
    return [tap_value / tap_total for tap_value in raw_taps]


def smooth_axis(padded, axis):
    weights = tap_weights()
    length = padded.shape[axis] - 8
    summed = jnp.zeros(padded.shape[:axis] + (length,) + padded.shape[axis + 1 :], jnp.float32)
    for offset in range(9):
        summed = summed + weights[offset] * lax.slice_in_dim(
            padded, offset, offset + length, axis=axis
        )
    return summed


def pad_axis(field, axis):
    widths = [(0, 0)] * field.ndim
    widths[axis] = (4, 4)
    return jnp.pad(field, widths)


def lookup(indices, table):
    hits = indices[:, None] == jnp.arange(table.shape[0], dtype=jnp.int32)[None, :]
    return jnp.sum(jnp.where(hits, table[None, :], 0), axis=1)


def pack_kernel(src_ref, pair_ref, fwd_ref, out_ref):
    dests = out_ref.shape[0]
    rows = fwd_ref.shape[1] * fwd_ref.shape[2] // LANES
    base = pl.program_id(0) * dests * 2

    def one_dest(d, carry):
        slot = base + 2 * d
        first = src_ref[slot]
        second = src_ref[slot + 1]
        out_ref[d, 0:rows, :] = fwd_ref[jnp.maximum(first, 0)].reshape(rows, LANES)
        out_ref[d, rows : 2 * rows, :] = fwd_ref[jnp.maximum(second, 0)].reshape(rows, LANES)
        lane_at = lax.broadcasted_iota(jnp.int32, (META, LANES), 1)
        tags = jnp.where(lane_at == 0, pair_ref[slot], pair_ref[slot + 1])
        out_ref[d, 2 * rows : 2 * rows + META, :] = tags.astype(jnp.float32).astype(out_ref.dtype)
        return carry

    lax.fori_loop(0, dests, one_dest, 0)


def correlate_kernel(pair_ref, arrived_ref, adj_ref, out_ref):
    dests = arrived_ref.shape[0]
    rows = adj_ref.shape[2]
    bricks = adj_ref.shape[1]
    groups = rows // 8
    base = pl.program_id(0) * dests * 2

    def one_slot(d, s):
        k = 2 * d + s
        pair = pair_ref[base + k]
        held = jnp.maximum(pair, 0)
        fwd = arrived_ref[d, s * rows : (s + 1) * rows, :].astype(jnp.float32)
        adj = adj_ref[held // bricks, held % bricks].astype(jnp.float32)
        prod = (fwd * adj).reshape(groups, 8, LANES)
        horizontal = None
        vertical = None
        for g in range(groups):
            if g % 3 == 2:
                vertical = prod[g] if vertical is None else vertical + prod[g]
            else:
                horizontal = prod[g] if horizontal is None else horizontal + prod[g]
        out_ref[k, 0] = jnp.where(pair >= 0, horizontal, 0.0)
        out_ref[k, 1] = jnp.where(pair >= 0, vertical, 0.0)

    for d in range(dests):
        one_slot(d, 0)
        one_slot(d, 1)


def src_sum(part):
    count = lax.axis_size("src")
    me = lax.axis_index("src")
    parts = [part] + [
        lax.ppermute(part, "src", [(i, (i + k) % count) for i in range(count)])
        for k in range(1, count)
    ]
    stacked = jnp.stack(parts)
    total = lax.dynamic_index_in_dim(stacked, me % count, keepdims=False)
    for j in range(1, count):
        total = total + lax.dynamic_index_in_dim(stacked, (me - j) % count, keepdims=False)
    return total


def local(forward, item_tx, item_brick, tx_place, brick_place, adjoint):
    stored = forward.shape[0]
    channels = forward.shape[1]
    cells = forward.shape[2]
    rows = channels * cells // LANES
    src_count = lax.axis_size("src")
    vol_count = lax.axis_size("vol")
    devices = src_count * vol_count
    local_tx = adjoint.shape[0]
    local_bricks = adjoint.shape[1]
    capacity = 2
    slot_total = devices * capacity
    tx_at = lookup(item_tx, tx_place)
    brick_at = lookup(item_brick, brick_place)
    destination = tx_at // local_tx * vol_count + brick_at // local_bricks
    pair_index = tx_at % local_tx * local_bricks + brick_at % local_bricks
    positions = jnp.arange(stored, dtype=jnp.int32)
    same_owner = destination[:, None] == destination[None, :]
    earlier = positions[:, None] > positions[None, :]
    order_rank = jnp.sum((same_owner & earlier).astype(jnp.int32), axis=1)
    slot_index = destination * capacity + order_rank
    slot_hits = slot_index[None, :] == jnp.arange(slot_total, dtype=jnp.int32)[:, None]
    filled = jnp.any(slot_hits, axis=1)
    src_of_slot = jnp.where(
        filled, jnp.sum(jnp.where(slot_hits, positions[None, :], 0), axis=1), -1
    ).astype(jnp.int32)
    pair_of_slot = jnp.where(
        filled, jnp.sum(jnp.where(slot_hits, pair_index[None, :], 0), axis=1), -1
    ).astype(jnp.int32)

    chunk = 2 * rows + META
    pack_steps = 8
    correlate_steps = 2
    dests_per_step = devices // pack_steps
    payload = pl.pallas_call(
        pack_kernel,
        out_shape=jax.ShapeDtypeStruct((devices, chunk, LANES), forward.dtype),
        grid_spec=pltpu.PrefetchScalarGridSpec(
            num_scalar_prefetch=2,
            grid=(pack_steps,),
            in_specs=[pl.BlockSpec((stored, channels, cells), lambda g, s, p: (0, 0, 0))],
            out_specs=pl.BlockSpec((dests_per_step, chunk, LANES), lambda g, s, p: (g, 0, 0)),
        ),
        compiler_params=pltpu.CompilerParams(vmem_limit_bytes=48 * 1024 * 1024),
    )(src_of_slot, pair_of_slot, forward)

    arrived = lax.all_to_all(payload, ("src", "vol"), split_axis=0, concat_axis=0, tiled=True)
    tags = arrived[:, 2 * rows, 0:2].reshape(slot_total)
    arrived_pairs = tags.astype(jnp.float32).astype(jnp.int32)

    adj_rows = jnp.transpose(
        jnp.transpose(adjoint, (0, 2, 1, 3)).reshape(local_tx, channels, local_bricks, cells // LANES, LANES),
        (0, 2, 1, 3, 4),
    ).reshape(local_tx, local_bricks, rows, LANES)
    per_slot = pl.pallas_call(
        correlate_kernel,
        out_shape=jax.ShapeDtypeStruct((slot_total, 2, 8, LANES), jnp.float32),
        grid_spec=pltpu.PrefetchScalarGridSpec(
            num_scalar_prefetch=1,
            grid=(correlate_steps,),
            in_specs=[
                pl.BlockSpec((devices // correlate_steps, chunk, LANES), lambda g, p: (g, 0, 0)),
                pl.BlockSpec((local_tx, local_bricks, rows, LANES), lambda g, p: (0, 0, 0, 0)),
            ],
            out_specs=pl.BlockSpec((2 * devices // correlate_steps, 2, 8, LANES), lambda g, p: (g, 0, 0, 0)),
        ),
        compiler_params=pltpu.CompilerParams(vmem_limit_bytes=48 * 1024 * 1024),
    )(arrived_pairs, arrived, adj_rows)

    corr = (per_slot[:, :, 0:4, :] - per_slot[:, :, 4:8, :]).reshape(slot_total, 2 * cells)
    owner_brick = jnp.maximum(arrived_pairs, 0) % local_bricks
    owner_table = (
        (owner_brick[None, :] == jnp.arange(local_bricks, dtype=jnp.int32)[:, None])
        & (arrived_pairs >= 0)[None, :]
    ).astype(jnp.float32)
    gradient = jnp.dot(owner_table, corr, precision=lax.Precision.HIGHEST).reshape(local_bricks, 2, cells)
    slab = (
        gradient.reshape(NBY, NBZ, 2, E, E, E)
        .transpose(2, 3, 0, 4, 1, 5)
        .reshape(2, E, NBY * E, NBZ * E)
    )
    summed = src_sum(slab)
    padded = with_halo(summed, (("vol", 1),), 4)
    field = smooth_axis(padded, 1)
    for axis in (2, 3):
        field = smooth_axis(pad_axis(field, axis), axis)
    return field


def solution(mesh):
    in_specs = (
        P(("src", "vol"), None, None),
        P(("src", "vol")),
        P(("src", "vol")),
        P(),
        P(),
        P("src", "vol", None, None),
    )
    out_specs = P(None, "vol", None, None)
    return jax.shard_map(local, mesh=mesh, in_specs=in_specs, out_specs=out_specs, check_vma=False)
```

```python
import math

import jax
import jax.numpy as jnp
from jax import lax
from jax.experimental import pallas as pl
from jax.experimental.pallas import tpu as pltpu
from jax.sharding import PartitionSpec as P

E = 8
NFREQ = 6
NBY = 2
NBZ = 16
LANES = 128
META = 16


def with_halo(cells, sides, width):
    for axis, dim in sides:
        count = lax.axis_size(axis)
        ends = count - 1
        head = lax.slice_in_dim(cells, 0, width, axis=dim)
        tail = lax.slice_in_dim(cells, cells.shape[dim] - width, cells.shape[dim], axis=dim)
        cells = jnp.concatenate(
            [
                lax.ppermute(tail, axis, [(i, (i + 1) % count) for i in range(ends)]),
                cells,
                lax.ppermute(head, axis, [((i + 1) % count, i) for i in range(ends)]),
            ],
            axis=dim,
        )
    return cells


def tap_weights():
    raw_taps = [math.exp(-(offset - 4) * (offset - 4) / 4.5) for offset in range(9)]
    tap_total = sum(raw_taps)
    return [tap_value / tap_total for tap_value in raw_taps]


def smooth_axis(padded, axis):
    weights = tap_weights()
    length = padded.shape[axis] - 8
    summed = jnp.zeros(padded.shape[:axis] + (length,) + padded.shape[axis + 1 :], jnp.float32)
    for offset in range(9):
        summed = summed + weights[offset] * lax.slice_in_dim(
            padded, offset, offset + length, axis=axis
        )
    return summed


def pad_axis(field, axis):
    widths = [(0, 0)] * field.ndim
    widths[axis] = (4, 4)
    return jnp.pad(field, widths)


def lookup(indices, table):
    hits = indices[:, None] == jnp.arange(table.shape[0], dtype=jnp.int32)[None, :]
    return jnp.sum(jnp.where(hits, table[None, :], 0), axis=1)


def pack_kernel(src_ref, pair_ref, fwd_ref, out_ref, bricks_ref):
    dests = out_ref.shape[0]
    rows = bricks_ref.shape[1]
    group = 16
    base = pl.program_id(0) * dests * 2

    @pl.when(pl.program_id(0) == 0)
    def _():
        for start in range(0, bricks_ref.shape[0], group):
            block = jnp.swapaxes(fwd_ref[:, start : start + group, :], 0, 1)
            for j in range(group):
                bricks_ref[start + j] = block[j].reshape(rows, LANES)

    def one_dest(d, carry):
        slot = base + 2 * d
        first = src_ref[slot]
        second = src_ref[slot + 1]
        out_ref[d, 0:rows, :] = bricks_ref[jnp.maximum(first, 0)]
        out_ref[d, rows : 2 * rows, :] = bricks_ref[jnp.maximum(second, 0)]
        lane_at = lax.broadcasted_iota(jnp.int32, (META, LANES), 1)
        tags = jnp.where(lane_at == 0, pair_ref[slot], pair_ref[slot + 1])
        out_ref[d, 2 * rows : 2 * rows + META, :] = tags.astype(jnp.float32).astype(out_ref.dtype)
        return carry

    lax.fori_loop(0, dests, one_dest, 0)


def correlate_kernel(pair_ref, arrived_ref, adj_ref, out_ref):
    dests = arrived_ref.shape[0]
    rows = adj_ref.shape[2]
    bricks = adj_ref.shape[1]
    groups = rows // 8
    base = pl.program_id(0) * dests * 2

    def one_slot(d, s):
        k = 2 * d + s
        pair = pair_ref[base + k]
        held = jnp.maximum(pair, 0)
        fwd = arrived_ref[d, s * rows : (s + 1) * rows, :].astype(jnp.float32)
        adj = adj_ref[held // bricks, held % bricks].astype(jnp.float32)
        prod = (fwd * adj).reshape(groups, 8, LANES)
        horizontal = None
        vertical = None
        for g in range(groups):
            if g % 3 == 2:
                vertical = prod[g] if vertical is None else vertical + prod[g]
            else:
                horizontal = prod[g] if horizontal is None else horizontal + prod[g]
        out_ref[k, 0] = jnp.where(pair >= 0, horizontal, 0.0)
        out_ref[k, 1] = jnp.where(pair >= 0, vertical, 0.0)

    for d in range(dests):
        one_slot(d, 0)
        one_slot(d, 1)


def src_sum(part):
    count = lax.axis_size("src")
    me = lax.axis_index("src")
    parts = [part] + [
        lax.ppermute(part, "src", [(i, (i + k) % count) for i in range(count)])
        for k in range(1, count)
    ]
    stacked = jnp.stack(parts)
    total = lax.dynamic_index_in_dim(stacked, me % count, keepdims=False)
    for j in range(1, count):
        total = total + lax.dynamic_index_in_dim(stacked, (me - j) % count, keepdims=False)
    return total


def local(forward, item_tx, item_brick, tx_place, brick_place, adjoint):
    stored = forward.shape[0]
    channels = forward.shape[1]
    cells = forward.shape[2]
    rows = channels * cells // LANES
    src_count = lax.axis_size("src")
    vol_count = lax.axis_size("vol")
    devices = src_count * vol_count
    local_tx = adjoint.shape[0]
    local_bricks = adjoint.shape[1]
    capacity = 2
    slot_total = devices * capacity
    tx_at = lookup(item_tx, tx_place)
    brick_at = lookup(item_brick, brick_place)
    destination = tx_at // local_tx * vol_count + brick_at // local_bricks
    pair_index = tx_at % local_tx * local_bricks + brick_at % local_bricks
    positions = jnp.arange(stored, dtype=jnp.int32)
    same_owner = destination[:, None] == destination[None, :]
    earlier = positions[:, None] > positions[None, :]
    order_rank = jnp.sum((same_owner & earlier).astype(jnp.int32), axis=1)
    slot_index = destination * capacity + order_rank
    slot_hits = slot_index[None, :] == jnp.arange(slot_total, dtype=jnp.int32)[:, None]
    filled = jnp.any(slot_hits, axis=1)
    src_of_slot = jnp.where(
        filled, jnp.sum(jnp.where(slot_hits, positions[None, :], 0), axis=1), -1
    ).astype(jnp.int32)
    pair_of_slot = jnp.where(
        filled, jnp.sum(jnp.where(slot_hits, pair_index[None, :], 0), axis=1), -1
    ).astype(jnp.int32)

    chunk = 2 * rows + META
    pack_steps = 8
    correlate_steps = 2
    dests_per_step = devices // pack_steps
    payload = pl.pallas_call(
        pack_kernel,
        out_shape=jax.ShapeDtypeStruct((devices, chunk, LANES), forward.dtype),
        grid_spec=pltpu.PrefetchScalarGridSpec(
            num_scalar_prefetch=2,
            grid=(pack_steps,),
            in_specs=[pl.BlockSpec((channels, stored, cells), lambda g, s, p: (0, 0, 0))],
            out_specs=pl.BlockSpec((dests_per_step, chunk, LANES), lambda g, s, p: (g, 0, 0)),
            scratch_shapes=[pltpu.VMEM((stored, rows, LANES), forward.dtype)],
        ),
        compiler_params=pltpu.CompilerParams(vmem_limit_bytes=48 * 1024 * 1024),
    )(src_of_slot, pair_of_slot, jnp.transpose(forward, (1, 0, 2)))

    arrived = lax.all_to_all(payload, ("src", "vol"), split_axis=0, concat_axis=0, tiled=True)
    tags = arrived[:, 2 * rows, 0:2].reshape(slot_total)
    arrived_pairs = tags.astype(jnp.float32).astype(jnp.int32)

    adj_rows = jnp.transpose(
        jnp.transpose(adjoint, (0, 2, 1, 3)).reshape(local_tx, channels, local_bricks, cells // LANES, LANES),
        (0, 2, 1, 3, 4),
    ).reshape(local_tx, local_bricks, rows, LANES)
    per_slot = pl.pallas_call(
        correlate_kernel,
        out_shape=jax.ShapeDtypeStruct((slot_total, 2, 8, LANES), jnp.float32),
        grid_spec=pltpu.PrefetchScalarGridSpec(
            num_scalar_prefetch=1,
            grid=(correlate_steps,),
            in_specs=[
                pl.BlockSpec((devices // correlate_steps, chunk, LANES), lambda g, p: (g, 0, 0)),
                pl.BlockSpec((local_tx, local_bricks, rows, LANES), lambda g, p: (0, 0, 0, 0)),
            ],
            out_specs=pl.BlockSpec((2 * devices // correlate_steps, 2, 8, LANES), lambda g, p: (g, 0, 0, 0)),
        ),
        compiler_params=pltpu.CompilerParams(vmem_limit_bytes=48 * 1024 * 1024),
    )(arrived_pairs, arrived, adj_rows)

    corr = (per_slot[:, :, 0:4, :] - per_slot[:, :, 4:8, :]).reshape(slot_total, 2 * cells)
    owner_brick = jnp.maximum(arrived_pairs, 0) % local_bricks
    owner_table = (
        (owner_brick[None, :] == jnp.arange(local_bricks, dtype=jnp.int32)[:, None])
        & (arrived_pairs >= 0)[None, :]
    ).astype(jnp.float32)
    gradient = jnp.dot(owner_table, corr, precision=lax.Precision.HIGHEST).reshape(local_bricks, 2, cells)
    slab = (
        gradient.reshape(NBY, NBZ, 2, E, E, E)
        .transpose(2, 3, 0, 4, 1, 5)
        .reshape(2, E, NBY * E, NBZ * E)
    )
    summed = src_sum(slab)
    padded = with_halo(summed, (("vol", 1),), 4)
    field = smooth_axis(padded, 1)
    for axis in (2, 3):
        field = smooth_axis(pad_axis(field, axis), axis)
    return field


def solution(mesh):
    in_specs = (
        P(("src", "vol"), None, None),
        P(("src", "vol")),
        P(("src", "vol")),
        P(),
        P(),
        P("src", "vol", None, None),
    )
    out_specs = P(None, "vol", None, None)
    return jax.shard_map(local, mesh=mesh, in_specs=in_specs, out_specs=out_specs, check_vma=False)
```

```python
import math

import jax
import jax.numpy as jnp
from jax import lax
from jax.experimental import pallas as pl
from jax.experimental.pallas import tpu as pltpu
from jax.sharding import PartitionSpec as P

E = 8
NFREQ = 6
NBY = 2
NBZ = 16
LANES = 128
META = 16


def with_halo(cells, sides, width):
    for axis, dim in sides:
        count = lax.axis_size(axis)
        ends = count - 1
        head = lax.slice_in_dim(cells, 0, width, axis=dim)
        tail = lax.slice_in_dim(cells, cells.shape[dim] - width, cells.shape[dim], axis=dim)
        cells = jnp.concatenate(
            [
                lax.ppermute(tail, axis, [(i, (i + 1) % count) for i in range(ends)]),
                cells,
                lax.ppermute(head, axis, [((i + 1) % count, i) for i in range(ends)]),
            ],
            axis=dim,
        )
    return cells


def tap_weights():
    raw_taps = [math.exp(-(offset - 4) * (offset - 4) / 4.5) for offset in range(9)]
    tap_total = sum(raw_taps)
    return [tap_value / tap_total for tap_value in raw_taps]


def smooth_axis(padded, axis):
    weights = tap_weights()
    length = padded.shape[axis] - 8
    summed = jnp.zeros(padded.shape[:axis] + (length,) + padded.shape[axis + 1 :], jnp.float32)
    for offset in range(9):
        summed = summed + weights[offset] * lax.slice_in_dim(
            padded, offset, offset + length, axis=axis
        )
    return summed


def pad_axis(field, axis):
    widths = [(0, 0)] * field.ndim
    widths[axis] = (4, 4)
    return jnp.pad(field, widths)


def lookup(indices, table):
    hits = indices[:, None] == jnp.arange(table.shape[0], dtype=jnp.int32)[None, :]
    return jnp.sum(jnp.where(hits, table[None, :], 0), axis=1)


def pack_kernel(src_ref, pair_ref, fwd_ref, out_ref, bricks_ref):
    dests = out_ref.shape[0]
    rows = bricks_ref.shape[1]
    group = 16
    base = pl.program_id(0) * dests * 2

    @pl.when(pl.program_id(0) == 0)
    def _():
        for start in range(0, bricks_ref.shape[0], group):
            block = jnp.swapaxes(fwd_ref[:, start : start + group, :], 0, 1)
            for j in range(group):
                bricks_ref[start + j] = block[j].reshape(rows, LANES)

    def one_dest(d, carry):
        slot = base + 2 * d
        first = src_ref[slot]
        second = src_ref[slot + 1]
        out_ref[d, 0:rows, :] = bricks_ref[jnp.maximum(first, 0)]
        out_ref[d, rows : 2 * rows, :] = bricks_ref[jnp.maximum(second, 0)]
        lane_at = lax.broadcasted_iota(jnp.int32, (META, LANES), 1)
        tags = jnp.where(lane_at == 0, pair_ref[slot], pair_ref[slot + 1])
        out_ref[d, 2 * rows : 2 * rows + META, :] = tags.astype(jnp.float32).astype(out_ref.dtype)
        return carry

    lax.fori_loop(0, dests, one_dest, 0, unroll=True)


def correlate_kernel(pair_ref, arrived_ref, adj_ref, out_ref):
    dests = arrived_ref.shape[0]
    rows = adj_ref.shape[2]
    bricks = adj_ref.shape[1]
    groups = rows // 8
    base = pl.program_id(0) * dests * 2

    def one_slot(d, s):
        k = 2 * d + s
        pair = pair_ref[base + k]
        held = jnp.maximum(pair, 0)
        fwd = arrived_ref[d, s * rows : (s + 1) * rows, :].astype(jnp.float32)
        adj = adj_ref[held // bricks, held % bricks].astype(jnp.float32)
        prod = (fwd * adj).reshape(groups, 8, LANES)
        horizontal = None
        vertical = None
        for g in range(groups):
            if g % 3 == 2:
                vertical = prod[g] if vertical is None else vertical + prod[g]
            else:
                horizontal = prod[g] if horizontal is None else horizontal + prod[g]
        out_ref[k, 0] = jnp.where(pair >= 0, horizontal, 0.0)
        out_ref[k, 1] = jnp.where(pair >= 0, vertical, 0.0)

    for d in range(dests):
        one_slot(d, 0)
        one_slot(d, 1)


def src_sum(part):
    count = lax.axis_size("src")
    me = lax.axis_index("src")
    parts = [part] + [
        lax.ppermute(part, "src", [(i, (i + k) % count) for i in range(count)])
        for k in range(1, count)
    ]
    stacked = jnp.stack(parts)
    total = lax.dynamic_index_in_dim(stacked, me % count, keepdims=False)
    for j in range(1, count):
        total = total + lax.dynamic_index_in_dim(stacked, (me - j) % count, keepdims=False)
    return total


def local(forward, item_tx, item_brick, tx_place, brick_place, adjoint):
    stored = forward.shape[0]
    channels = forward.shape[1]
    cells = forward.shape[2]
    rows = channels * cells // LANES
    src_count = lax.axis_size("src")
    vol_count = lax.axis_size("vol")
    devices = src_count * vol_count
    local_tx = adjoint.shape[0]
    local_bricks = adjoint.shape[1]
    capacity = 2
    slot_total = devices * capacity
    tx_at = lookup(item_tx, tx_place)
    brick_at = lookup(item_brick, brick_place)
    destination = tx_at // local_tx * vol_count + brick_at // local_bricks
    pair_index = tx_at % local_tx * local_bricks + brick_at % local_bricks
    positions = jnp.arange(stored, dtype=jnp.int32)
    same_owner = destination[:, None] == destination[None, :]
    earlier = positions[:, None] > positions[None, :]
    order_rank = jnp.sum((same_owner & earlier).astype(jnp.int32), axis=1)
    slot_index = destination * capacity + order_rank
    slot_hits = slot_index[None, :] == jnp.arange(slot_total, dtype=jnp.int32)[:, None]
    filled = jnp.any(slot_hits, axis=1)
    src_of_slot = jnp.where(
        filled, jnp.sum(jnp.where(slot_hits, positions[None, :], 0), axis=1), -1
    ).astype(jnp.int32)
    pair_of_slot = jnp.where(
        filled, jnp.sum(jnp.where(slot_hits, pair_index[None, :], 0), axis=1), -1
    ).astype(jnp.int32)

    chunk = 2 * rows + META
    pack_steps = 8
    correlate_steps = 2
    dests_per_step = devices // pack_steps
    payload = pl.pallas_call(
        pack_kernel,
        out_shape=jax.ShapeDtypeStruct((devices, chunk, LANES), forward.dtype),
        grid_spec=pltpu.PrefetchScalarGridSpec(
            num_scalar_prefetch=2,
            grid=(pack_steps,),
            in_specs=[pl.BlockSpec((channels, stored, cells), lambda g, s, p: (0, 0, 0))],
            out_specs=pl.BlockSpec((dests_per_step, chunk, LANES), lambda g, s, p: (g, 0, 0)),
            scratch_shapes=[pltpu.VMEM((stored, rows, LANES), forward.dtype)],
        ),
        compiler_params=pltpu.CompilerParams(vmem_limit_bytes=48 * 1024 * 1024),
    )(src_of_slot, pair_of_slot, jnp.transpose(forward, (1, 0, 2)))

    arrived = lax.all_to_all(payload, ("src", "vol"), split_axis=0, concat_axis=0, tiled=True)
    tags = arrived[:, 2 * rows, 0:2].reshape(slot_total)
    arrived_pairs = tags.astype(jnp.float32).astype(jnp.int32)

    adj_rows = jnp.transpose(
        jnp.transpose(adjoint, (0, 2, 1, 3)).reshape(local_tx, channels, local_bricks, cells // LANES, LANES),
        (0, 2, 1, 3, 4),
    ).reshape(local_tx, local_bricks, rows, LANES)
    per_slot = pl.pallas_call(
        correlate_kernel,
        out_shape=jax.ShapeDtypeStruct((slot_total, 2, 8, LANES), jnp.float32),
        grid_spec=pltpu.PrefetchScalarGridSpec(
            num_scalar_prefetch=1,
            grid=(correlate_steps,),
            in_specs=[
                pl.BlockSpec((devices // correlate_steps, chunk, LANES), lambda g, p: (g, 0, 0)),
                pl.BlockSpec((local_tx, local_bricks, rows, LANES), lambda g, p: (0, 0, 0, 0)),
            ],
            out_specs=pl.BlockSpec((2 * devices // correlate_steps, 2, 8, LANES), lambda g, p: (g, 0, 0, 0)),
        ),
        compiler_params=pltpu.CompilerParams(vmem_limit_bytes=48 * 1024 * 1024),
    )(arrived_pairs, arrived, adj_rows)

    corr = (per_slot[:, :, 0:4, :] - per_slot[:, :, 4:8, :]).reshape(slot_total, 2 * cells)
    owner_brick = jnp.maximum(arrived_pairs, 0) % local_bricks
    owner_table = (
        (owner_brick[None, :] == jnp.arange(local_bricks, dtype=jnp.int32)[:, None])
        & (arrived_pairs >= 0)[None, :]
    ).astype(jnp.float32)
    gradient = jnp.dot(owner_table, corr, precision=lax.Precision.HIGHEST).reshape(local_bricks, 2, cells)
    slab = (
        gradient.reshape(NBY, NBZ, 2, E, E, E)
        .transpose(2, 3, 0, 4, 1, 5)
        .reshape(2, E, NBY * E, NBZ * E)
    )
    summed = src_sum(slab)
    padded = with_halo(summed, (("vol", 1),), 4)
    field = smooth_axis(padded, 1)
    for axis in (2, 3):
        field = smooth_axis(pad_axis(field, axis), axis)
    return field


def solution(mesh):
    in_specs = (
        P(("src", "vol"), None, None),
        P(("src", "vol")),
        P(("src", "vol")),
        P(),
        P(),
        P("src", "vol", None, None),
    )
    out_specs = P(None, "vol", None, None)
    return jax.shard_map(local, mesh=mesh, in_specs=in_specs, out_specs=out_specs, check_vma=False)
```

```python
import math

import jax
import jax.numpy as jnp
from jax import lax
from jax.experimental import pallas as pl
from jax.experimental.pallas import tpu as pltpu
from jax.sharding import PartitionSpec as P

E = 8
NFREQ = 6
NBY = 2
NBZ = 16
LANES = 128
META = 16


def with_halo(cells, sides, width):
    for axis, dim in sides:
        count = lax.axis_size(axis)
        ends = count - 1
        head = lax.slice_in_dim(cells, 0, width, axis=dim)
        tail = lax.slice_in_dim(cells, cells.shape[dim] - width, cells.shape[dim], axis=dim)
        cells = jnp.concatenate(
            [
                lax.ppermute(tail, axis, [(i, (i + 1) % count) for i in range(ends)]),
                cells,
                lax.ppermute(head, axis, [((i + 1) % count, i) for i in range(ends)]),
            ],
            axis=dim,
        )
    return cells


def tap_weights():
    raw_taps = [math.exp(-(offset - 4) * (offset - 4) / 4.5) for offset in range(9)]
    tap_total = sum(raw_taps)
    return [tap_value / tap_total for tap_value in raw_taps]


def smooth_axis(padded, axis):
    weights = tap_weights()
    length = padded.shape[axis] - 8
    summed = jnp.zeros(padded.shape[:axis] + (length,) + padded.shape[axis + 1 :], jnp.float32)
    for offset in range(9):
        summed = summed + weights[offset] * lax.slice_in_dim(
            padded, offset, offset + length, axis=axis
        )
    return summed


def pad_axis(field, axis):
    widths = [(0, 0)] * field.ndim
    widths[axis] = (4, 4)
    return jnp.pad(field, widths)


def lookup(indices, table):
    hits = indices[:, None] == jnp.arange(table.shape[0], dtype=jnp.int32)[None, :]
    return jnp.sum(jnp.where(hits, table[None, :], 0), axis=1)


def pack_kernel(src_ref, pair_ref, fwd_ref, out_ref, bricks_ref):
    dests = out_ref.shape[0]
    rows = bricks_ref.shape[1]
    group = 16
    base = pl.program_id(0) * dests * 2

    @pl.when(pl.program_id(0) == 0)
    def _():
        for start in range(0, bricks_ref.shape[0], group):
            block = jnp.swapaxes(fwd_ref[:, start : start + group, :], 0, 1)
            for j in range(group):
                bricks_ref[start + j] = block[j].reshape(rows, LANES)

    def one_dest(d, carry):
        slot = base + 2 * d
        first = src_ref[slot]
        second = src_ref[slot + 1]
        out_ref[d, 0:rows, :] = bricks_ref[jnp.maximum(first, 0)]
        out_ref[d, rows : 2 * rows, :] = bricks_ref[jnp.maximum(second, 0)]
        lane_at = lax.broadcasted_iota(jnp.int32, (META, LANES), 1)
        tags = jnp.where(lane_at == 0, pair_ref[slot], pair_ref[slot + 1])
        out_ref[d, 2 * rows : 2 * rows + META, :] = tags.astype(jnp.float32).astype(out_ref.dtype)
        return carry

    lax.fori_loop(0, dests, one_dest, 0, unroll=True)


def correlate_kernel(pair_ref, arrived_ref, adj_ref, out_ref):
    dests = arrived_ref.shape[0]
    rows = adj_ref.shape[2]
    bricks = adj_ref.shape[1]
    groups = rows // 8
    base = pl.program_id(0) * dests * 2

    def one_slot(d, s):
        k = 2 * d + s
        pair = pair_ref[base + k]
        held = jnp.maximum(pair, 0)
        fwd = arrived_ref[d, s * rows : (s + 1) * rows, :].astype(jnp.float32)
        adj = adj_ref[held // bricks, held % bricks].astype(jnp.float32)
        prod = (fwd * adj).reshape(groups, 8, LANES)
        horizontal = None
        vertical = None
        for g in range(groups):
            if g % 3 == 2:
                vertical = prod[g] if vertical is None else vertical + prod[g]
            else:
                horizontal = prod[g] if horizontal is None else horizontal + prod[g]
        out_ref[k, 0] = jnp.where(pair >= 0, horizontal, 0.0)
        out_ref[k, 1] = jnp.where(pair >= 0, vertical, 0.0)

    for d in range(dests):
        one_slot(d, 0)
        one_slot(d, 1)


def src_sum(part):
    count = lax.axis_size("src")
    total = part
    step = 1
    while step < count:
        total = total + lax.ppermute(total, "src", [(i, i ^ step) for i in range(count)])
        step *= 2
    return total


def local(forward, item_tx, item_brick, tx_place, brick_place, adjoint):
    stored = forward.shape[0]
    channels = forward.shape[1]
    cells = forward.shape[2]
    rows = channels * cells // LANES
    src_count = lax.axis_size("src")
    vol_count = lax.axis_size("vol")
    devices = src_count * vol_count
    local_tx = adjoint.shape[0]
    local_bricks = adjoint.shape[1]
    capacity = 2
    slot_total = devices * capacity
    tx_at = lookup(item_tx, tx_place)
    brick_at = lookup(item_brick, brick_place)
    destination = tx_at // local_tx * vol_count + brick_at // local_bricks
    pair_index = tx_at % local_tx * local_bricks + brick_at % local_bricks
    positions = jnp.arange(stored, dtype=jnp.int32)
    same_owner = destination[:, None] == destination[None, :]
    earlier = positions[:, None] > positions[None, :]
    order_rank = jnp.sum((same_owner & earlier).astype(jnp.int32), axis=1)
    slot_index = destination * capacity + order_rank
    slot_hits = slot_index[None, :] == jnp.arange(slot_total, dtype=jnp.int32)[:, None]
    filled = jnp.any(slot_hits, axis=1)
    src_of_slot = jnp.where(
        filled, jnp.sum(jnp.where(slot_hits, positions[None, :], 0), axis=1), -1
    ).astype(jnp.int32)
    pair_of_slot = jnp.where(
        filled, jnp.sum(jnp.where(slot_hits, pair_index[None, :], 0), axis=1), -1
    ).astype(jnp.int32)

    chunk = 2 * rows + META
    pack_steps = 8
    correlate_steps = 2
    dests_per_step = devices // pack_steps
    payload = pl.pallas_call(
        pack_kernel,
        out_shape=jax.ShapeDtypeStruct((devices, chunk, LANES), forward.dtype),
        grid_spec=pltpu.PrefetchScalarGridSpec(
            num_scalar_prefetch=2,
            grid=(pack_steps,),
            in_specs=[pl.BlockSpec((channels, stored, cells), lambda g, s, p: (0, 0, 0))],
            out_specs=pl.BlockSpec((dests_per_step, chunk, LANES), lambda g, s, p: (g, 0, 0)),
            scratch_shapes=[pltpu.VMEM((stored, rows, LANES), forward.dtype)],
        ),
        compiler_params=pltpu.CompilerParams(vmem_limit_bytes=48 * 1024 * 1024),
    )(src_of_slot, pair_of_slot, jnp.transpose(forward, (1, 0, 2)))

    arrived = lax.all_to_all(payload, ("src", "vol"), split_axis=0, concat_axis=0, tiled=True)
    tags = arrived[:, 2 * rows, 0:2].reshape(slot_total)
    arrived_pairs = tags.astype(jnp.float32).astype(jnp.int32)

    adj_rows = jnp.transpose(
        jnp.transpose(adjoint, (0, 2, 1, 3)).reshape(local_tx, channels, local_bricks, cells // LANES, LANES),
        (0, 2, 1, 3, 4),
    ).reshape(local_tx, local_bricks, rows, LANES)
    per_slot = pl.pallas_call(
        correlate_kernel,
        out_shape=jax.ShapeDtypeStruct((slot_total, 2, 8, LANES), jnp.float32),
        grid_spec=pltpu.PrefetchScalarGridSpec(
            num_scalar_prefetch=1,
            grid=(correlate_steps,),
            in_specs=[
                pl.BlockSpec((devices // correlate_steps, chunk, LANES), lambda g, p: (g, 0, 0)),
                pl.BlockSpec((local_tx, local_bricks, rows, LANES), lambda g, p: (0, 0, 0, 0)),
            ],
            out_specs=pl.BlockSpec((2 * devices // correlate_steps, 2, 8, LANES), lambda g, p: (g, 0, 0, 0)),
        ),
        compiler_params=pltpu.CompilerParams(vmem_limit_bytes=48 * 1024 * 1024),
    )(arrived_pairs, arrived, adj_rows)

    corr = (per_slot[:, :, 0:4, :] - per_slot[:, :, 4:8, :]).reshape(slot_total, 2 * cells)
    owner_brick = jnp.maximum(arrived_pairs, 0) % local_bricks
    owner_table = (
        (owner_brick[None, :] == jnp.arange(local_bricks, dtype=jnp.int32)[:, None])
        & (arrived_pairs >= 0)[None, :]
    ).astype(jnp.float32)
    gradient = jnp.dot(owner_table, corr, precision=lax.Precision.HIGHEST).reshape(local_bricks, 2, cells)
    slab = (
        gradient.reshape(NBY, NBZ, 2, E, E, E)
        .transpose(2, 3, 0, 4, 1, 5)
        .reshape(2, E, NBY * E, NBZ * E)
    )
    summed = src_sum(slab)
    padded = with_halo(summed, (("vol", 1),), 4)
    field = smooth_axis(padded, 1)
    for axis in (2, 3):
        field = smooth_axis(pad_axis(field, axis), axis)
    return field


def solution(mesh):
    in_specs = (
        P(("src", "vol"), None, None),
        P(("src", "vol")),
        P(("src", "vol")),
        P(),
        P(),
        P("src", "vol", None, None),
    )
    out_specs = P(None, "vol", None, None)
    return jax.shard_map(local, mesh=mesh, in_specs=in_specs, out_specs=out_specs, check_vma=False)
```

```python
import math

import jax
import jax.numpy as jnp
from jax import lax
from jax.experimental import pallas as pl
from jax.experimental.pallas import tpu as pltpu
from jax.sharding import PartitionSpec as P

E = 8
NFREQ = 6
NBY = 2
NBZ = 16
LANES = 128
META = 16


def with_halo(cells, sides, width):
    for axis, dim in sides:
        count = lax.axis_size(axis)
        ends = count - 1
        head = lax.slice_in_dim(cells, 0, width, axis=dim)
        tail = lax.slice_in_dim(cells, cells.shape[dim] - width, cells.shape[dim], axis=dim)
        cells = jnp.concatenate(
            [
                lax.ppermute(tail, axis, [(i, (i + 1) % count) for i in range(ends)]),
                cells,
                lax.ppermute(head, axis, [((i + 1) % count, i) for i in range(ends)]),
            ],
            axis=dim,
        )
    return cells


def tap_weights():
    raw_taps = [math.exp(-(offset - 4) * (offset - 4) / 4.5) for offset in range(9)]
    tap_total = sum(raw_taps)
    return [tap_value / tap_total for tap_value in raw_taps]


def smooth_axis(padded, axis):
    weights = tap_weights()
    length = padded.shape[axis] - 8
    summed = jnp.zeros(padded.shape[:axis] + (length,) + padded.shape[axis + 1 :], jnp.float32)
    for offset in range(9):
        summed = summed + weights[offset] * lax.slice_in_dim(
            padded, offset, offset + length, axis=axis
        )
    return summed


def pad_axis(field, axis):
    widths = [(0, 0)] * field.ndim
    widths[axis] = (4, 4)
    return jnp.pad(field, widths)


def lookup(indices, table):
    hits = indices[:, None] == jnp.arange(table.shape[0], dtype=jnp.int32)[None, :]
    return jnp.sum(jnp.where(hits, table[None, :], 0), axis=1)


def pack_kernel(src_ref, pair_ref, fwd_ref, out_ref, bricks_ref):
    dests = out_ref.shape[0]
    rows = bricks_ref.shape[1]
    group = 16
    base = pl.program_id(0) * dests * 2

    @pl.when(pl.program_id(0) == 0)
    def _():
        for start in range(0, bricks_ref.shape[0], group):
            block = jnp.swapaxes(fwd_ref[:, start : start + group, :], 0, 1)
            for j in range(group):
                bricks_ref[start + j] = block[j].reshape(rows, LANES)

    def one_dest(d, carry):
        slot = base + 2 * d
        first = src_ref[slot]
        second = src_ref[slot + 1]
        out_ref[d, 0:rows, :] = bricks_ref[jnp.maximum(first, 0)]
        out_ref[d, rows : 2 * rows, :] = bricks_ref[jnp.maximum(second, 0)]
        lane_at = lax.broadcasted_iota(jnp.int32, (META, LANES), 1)
        tags = jnp.where(lane_at == 0, pair_ref[slot], pair_ref[slot + 1])
        out_ref[d, 2 * rows : 2 * rows + META, :] = tags.astype(jnp.float32).astype(out_ref.dtype)
        return carry

    lax.fori_loop(0, dests, one_dest, 0, unroll=True)


def correlate_kernel(pair_ref, arrived_ref, adj_ref, out_ref):
    dests = arrived_ref.shape[0]
    rows = adj_ref.shape[2]
    bricks = adj_ref.shape[1]
    groups = rows // 8
    base = pl.program_id(0) * dests * 2

    def one_slot(d, s):
        k = 2 * d + s
        pair = pair_ref[base + k]
        held = jnp.maximum(pair, 0)
        fwd = arrived_ref[d, s * rows : (s + 1) * rows, :].astype(jnp.float32)
        adj = adj_ref[held // bricks, held % bricks].astype(jnp.float32)
        prod = (fwd * adj).reshape(groups, 8, LANES)
        horizontal = None
        vertical = None
        for g in range(groups):
            if g % 3 == 2:
                vertical = prod[g] if vertical is None else vertical + prod[g]
            else:
                horizontal = prod[g] if horizontal is None else horizontal + prod[g]
        out_ref[k, 0] = jnp.where(pair >= 0, horizontal, 0.0)
        out_ref[k, 1] = jnp.where(pair >= 0, vertical, 0.0)

    for d in range(dests):
        one_slot(d, 0)
        one_slot(d, 1)


def src_sum(part):
    count = lax.axis_size("src")
    me = lax.axis_index("src")
    parts = [part] + [
        lax.ppermute(part, "src", [(i, (i + k) % count) for i in range(count)])
        for k in range(1, count)
    ]
    stacked = jnp.stack(parts)
    total = lax.dynamic_index_in_dim(stacked, me % count, keepdims=False)
    for j in range(1, count):
        total = total + lax.dynamic_index_in_dim(stacked, (me - j) % count, keepdims=False)
    return total


def local(forward, item_tx, item_brick, tx_place, brick_place, adjoint):
    stored = forward.shape[0]
    channels = forward.shape[1]
    cells = forward.shape[2]
    rows = channels * cells // LANES
    src_count = lax.axis_size("src")
    vol_count = lax.axis_size("vol")
    devices = src_count * vol_count
    local_tx = adjoint.shape[0]
    local_bricks = adjoint.shape[1]
    capacity = 2
    slot_total = devices * capacity
    tx_at = lookup(item_tx, tx_place)
    brick_at = lookup(item_brick, brick_place)
    destination = tx_at // local_tx * vol_count + brick_at // local_bricks
    pair_index = tx_at % local_tx * local_bricks + brick_at % local_bricks
    positions = jnp.arange(stored, dtype=jnp.int32)
    same_owner = destination[:, None] == destination[None, :]
    earlier = positions[:, None] > positions[None, :]
    order_rank = jnp.sum((same_owner & earlier).astype(jnp.int32), axis=1)
    slot_index = destination * capacity + order_rank
    slot_hits = slot_index[None, :] == jnp.arange(slot_total, dtype=jnp.int32)[:, None]
    filled = jnp.any(slot_hits, axis=1)
    src_of_slot = jnp.where(
        filled, jnp.sum(jnp.where(slot_hits, positions[None, :], 0), axis=1), -1
    ).astype(jnp.int32)
    pair_of_slot = jnp.where(
        filled, jnp.sum(jnp.where(slot_hits, pair_index[None, :], 0), axis=1), -1
    ).astype(jnp.int32)

    chunk = 2 * rows + META
    pack_steps = 8
    correlate_steps = 2
    dests_per_step = devices // pack_steps
    payload = pl.pallas_call(
        pack_kernel,
        out_shape=jax.ShapeDtypeStruct((devices, chunk, LANES), forward.dtype),
        grid_spec=pltpu.PrefetchScalarGridSpec(
            num_scalar_prefetch=2,
            grid=(pack_steps,),
            in_specs=[pl.BlockSpec((channels, stored, cells), lambda g, s, p: (0, 0, 0))],
            out_specs=pl.BlockSpec((dests_per_step, chunk, LANES), lambda g, s, p: (g, 0, 0)),
            scratch_shapes=[pltpu.VMEM((stored, rows, LANES), forward.dtype)],
        ),
        compiler_params=pltpu.CompilerParams(vmem_limit_bytes=48 * 1024 * 1024),
    )(src_of_slot, pair_of_slot, jnp.transpose(forward, (1, 0, 2)))

    arrived = lax.all_to_all(payload, ("src", "vol"), split_axis=0, concat_axis=0, tiled=True)
    tags = arrived[:, 2 * rows, 0:2].reshape(slot_total)
    arrived_pairs = tags.astype(jnp.float32).astype(jnp.int32)

    adj_rows = jnp.transpose(
        jnp.transpose(adjoint, (0, 2, 1, 3)).reshape(local_tx, channels, local_bricks, cells // LANES, LANES),
        (0, 2, 1, 3, 4),
    ).reshape(local_tx, local_bricks, rows, LANES)
    per_slot = pl.pallas_call(
        correlate_kernel,
        out_shape=jax.ShapeDtypeStruct((slot_total, 2, 8, LANES), jnp.float32),
        grid_spec=pltpu.PrefetchScalarGridSpec(
            num_scalar_prefetch=1,
            grid=(correlate_steps,),
            in_specs=[
                pl.BlockSpec((devices // correlate_steps, chunk, LANES), lambda g, p: (g, 0, 0)),
                pl.BlockSpec((local_tx, local_bricks, rows, LANES), lambda g, p: (0, 0, 0, 0)),
            ],
            out_specs=pl.BlockSpec((2 * devices // correlate_steps, 2, 8, LANES), lambda g, p: (g, 0, 0, 0)),
        ),
        compiler_params=pltpu.CompilerParams(vmem_limit_bytes=48 * 1024 * 1024),
    )(arrived_pairs, arrived, adj_rows)

    corr = (per_slot[:, :, 0:4, :] - per_slot[:, :, 4:8, :]).reshape(slot_total, 2 * cells)
    owner_brick = jnp.maximum(arrived_pairs, 0) % local_bricks
    owner_table = (
        (owner_brick[None, :] == jnp.arange(local_bricks, dtype=jnp.int32)[:, None])
        & (arrived_pairs >= 0)[None, :]
    ).astype(jnp.float32)
    gradient = jnp.dot(owner_table, corr, precision=lax.Precision.HIGHEST).reshape(local_bricks, 2, cells)
    slab = (
        gradient.reshape(NBY, NBZ, 2, E, E, E)
        .transpose(2, 3, 0, 4, 1, 5)
        .reshape(2, E, NBY * E, NBZ * E)
    )
    padded = src_sum(with_halo(slab, (("vol", 1),), 4))
    field = smooth_axis(padded, 1)
    for axis in (2, 3):
        field = smooth_axis(pad_axis(field, axis), axis)
    return field


def solution(mesh):
    in_specs = (
        P(("src", "vol"), None, None),
        P(("src", "vol")),
        P(("src", "vol")),
        P(),
        P(),
        P("src", "vol", None, None),
    )
    out_specs = P(None, "vol", None, None)
    return jax.shard_map(local, mesh=mesh, in_specs=in_specs, out_specs=out_specs, check_vma=False)
```

```python
import math

import jax
import jax.numpy as jnp
from jax import lax
from jax.experimental import pallas as pl
from jax.experimental.pallas import tpu as pltpu
from jax.sharding import PartitionSpec as P

E = 8
NFREQ = 6
NBY = 2
NBZ = 16
LANES = 128
META = 16


def with_halo(cells, sides, width):
    for axis, dim in sides:
        count = lax.axis_size(axis)
        ends = count - 1
        head = lax.slice_in_dim(cells, 0, width, axis=dim)
        tail = lax.slice_in_dim(cells, cells.shape[dim] - width, cells.shape[dim], axis=dim)
        cells = jnp.concatenate(
            [
                lax.ppermute(tail, axis, [(i, (i + 1) % count) for i in range(ends)]),
                cells,
                lax.ppermute(head, axis, [((i + 1) % count, i) for i in range(ends)]),
            ],
            axis=dim,
        )
    return cells


def tap_weights():
    raw_taps = [math.exp(-(offset - 4) * (offset - 4) / 4.5) for offset in range(9)]
    tap_total = sum(raw_taps)
    return [tap_value / tap_total for tap_value in raw_taps]


def smooth_axis(padded, axis):
    weights = tap_weights()
    length = padded.shape[axis] - 8
    summed = jnp.zeros(padded.shape[:axis] + (length,) + padded.shape[axis + 1 :], jnp.float32)
    for offset in range(9):
        summed = summed + weights[offset] * lax.slice_in_dim(
            padded, offset, offset + length, axis=axis
        )
    return summed


def pad_axis(field, axis):
    widths = [(0, 0)] * field.ndim
    widths[axis] = (4, 4)
    return jnp.pad(field, widths)


def lookup(indices, table):
    hits = indices[:, None] == jnp.arange(table.shape[0], dtype=jnp.int32)[None, :]
    return jnp.sum(jnp.where(hits, table[None, :], 0), axis=1)


def pack_kernel(src_ref, pair_ref, fwd_ref, out_ref, bricks_ref):
    dests = out_ref.shape[0]
    rows = bricks_ref.shape[1]
    group = 16
    base = pl.program_id(0) * dests * 2

    @pl.when(pl.program_id(0) == 0)
    def _():
        for start in range(0, bricks_ref.shape[0], group):
            block = jnp.swapaxes(fwd_ref[:, start : start + group, :], 0, 1)
            for j in range(group):
                bricks_ref[start + j] = block[j].reshape(rows, LANES)

    def one_dest(d, carry):
        slot = base + 2 * d
        first = src_ref[slot]
        second = src_ref[slot + 1]
        out_ref[d, 0:rows, :] = bricks_ref[jnp.maximum(first, 0)]
        out_ref[d, rows : 2 * rows, :] = bricks_ref[jnp.maximum(second, 0)]
        lane_at = lax.broadcasted_iota(jnp.int32, (META, LANES), 1)
        tags = jnp.where(lane_at == 0, pair_ref[slot], pair_ref[slot + 1])
        out_ref[d, 2 * rows : 2 * rows + META, :] = tags.astype(jnp.float32).astype(out_ref.dtype)
        return carry

    lax.fori_loop(0, dests, one_dest, 0, unroll=True)


def correlate_kernel(pair_ref, arrived_ref, adj_ref, out_ref):
    dests = arrived_ref.shape[0]
    rows = adj_ref.shape[2]
    bricks = adj_ref.shape[1]
    groups = rows // 8
    base = pl.program_id(0) * dests * 2

    def one_slot(d, s):
        k = 2 * d + s
        pair = pair_ref[base + k]
        held = jnp.maximum(pair, 0)
        fwd = arrived_ref[d, s * rows : (s + 1) * rows, :].astype(jnp.float32)
        adj = adj_ref[held // bricks, held % bricks].astype(jnp.float32)
        prod = (fwd * adj).reshape(groups, 8, LANES)
        horizontal = None
        vertical = None
        for g in range(groups):
            if g % 3 == 2:
                vertical = prod[g] if vertical is None else vertical + prod[g]
            else:
                horizontal = prod[g] if horizontal is None else horizontal + prod[g]
        brick = held % bricks
        out_ref[brick, 0] += jnp.where(pair >= 0, horizontal, 0.0)
        out_ref[brick, 1] += jnp.where(pair >= 0, vertical, 0.0)

    @pl.when(pl.program_id(0) == 0)
    def _():
        out_ref[...] = jnp.zeros(out_ref.shape, out_ref.dtype)

    for d in range(dests):
        one_slot(d, 0)
        one_slot(d, 1)


def src_sum(part):
    count = lax.axis_size("src")
    me = lax.axis_index("src")
    parts = [part] + [
        lax.ppermute(part, "src", [(i, (i + k) % count) for i in range(count)])
        for k in range(1, count)
    ]
    stacked = jnp.stack(parts)
    total = lax.dynamic_index_in_dim(stacked, me % count, keepdims=False)
    for j in range(1, count):
        total = total + lax.dynamic_index_in_dim(stacked, (me - j) % count, keepdims=False)
    return total


def local(forward, item_tx, item_brick, tx_place, brick_place, adjoint):
    stored = forward.shape[0]
    channels = forward.shape[1]
    cells = forward.shape[2]
    rows = channels * cells // LANES
    src_count = lax.axis_size("src")
    vol_count = lax.axis_size("vol")
    devices = src_count * vol_count
    local_tx = adjoint.shape[0]
    local_bricks = adjoint.shape[1]
    capacity = 2
    slot_total = devices * capacity
    tx_at = lookup(item_tx, tx_place)
    brick_at = lookup(item_brick, brick_place)
    destination = tx_at // local_tx * vol_count + brick_at // local_bricks
    pair_index = tx_at % local_tx * local_bricks + brick_at % local_bricks
    positions = jnp.arange(stored, dtype=jnp.int32)
    same_owner = destination[:, None] == destination[None, :]
    earlier = positions[:, None] > positions[None, :]
    order_rank = jnp.sum((same_owner & earlier).astype(jnp.int32), axis=1)
    slot_index = destination * capacity + order_rank
    slot_hits = slot_index[None, :] == jnp.arange(slot_total, dtype=jnp.int32)[:, None]
    filled = jnp.any(slot_hits, axis=1)
    src_of_slot = jnp.where(
        filled, jnp.sum(jnp.where(slot_hits, positions[None, :], 0), axis=1), -1
    ).astype(jnp.int32)
    pair_of_slot = jnp.where(
        filled, jnp.sum(jnp.where(slot_hits, pair_index[None, :], 0), axis=1), -1
    ).astype(jnp.int32)

    chunk = 2 * rows + META
    pack_steps = 8
    correlate_steps = 2
    dests_per_step = devices // pack_steps
    payload = pl.pallas_call(
        pack_kernel,
        out_shape=jax.ShapeDtypeStruct((devices, chunk, LANES), forward.dtype),
        grid_spec=pltpu.PrefetchScalarGridSpec(
            num_scalar_prefetch=2,
            grid=(pack_steps,),
            in_specs=[pl.BlockSpec((channels, stored, cells), lambda g, s, p: (0, 0, 0))],
            out_specs=pl.BlockSpec((dests_per_step, chunk, LANES), lambda g, s, p: (g, 0, 0)),
            scratch_shapes=[pltpu.VMEM((stored, rows, LANES), forward.dtype)],
        ),
        compiler_params=pltpu.CompilerParams(vmem_limit_bytes=48 * 1024 * 1024),
    )(src_of_slot, pair_of_slot, jnp.transpose(forward, (1, 0, 2)))

    arrived = lax.all_to_all(payload, ("src", "vol"), split_axis=0, concat_axis=0, tiled=True)
    tags = arrived[:, 2 * rows, 0:2].reshape(slot_total)
    arrived_pairs = tags.astype(jnp.float32).astype(jnp.int32)

    adj_rows = jnp.transpose(
        jnp.transpose(adjoint, (0, 2, 1, 3)).reshape(local_tx, channels, local_bricks, cells // LANES, LANES),
        (0, 2, 1, 3, 4),
    ).reshape(local_tx, local_bricks, rows, LANES)
    per_slot = pl.pallas_call(
        correlate_kernel,
        out_shape=jax.ShapeDtypeStruct((local_bricks, 2, 8, LANES), jnp.float32),
        grid_spec=pltpu.PrefetchScalarGridSpec(
            num_scalar_prefetch=1,
            grid=(correlate_steps,),
            in_specs=[
                pl.BlockSpec((devices // correlate_steps, chunk, LANES), lambda g, p: (g, 0, 0)),
                pl.BlockSpec((local_tx, local_bricks, rows, LANES), lambda g, p: (0, 0, 0, 0)),
            ],
            out_specs=pl.BlockSpec((local_bricks, 2, 8, LANES), lambda g, p: (0, 0, 0, 0)),
        ),
        compiler_params=pltpu.CompilerParams(vmem_limit_bytes=48 * 1024 * 1024),
    )(arrived_pairs, arrived, adj_rows)

    gradient = (per_slot[:, :, 0:4, :] - per_slot[:, :, 4:8, :]).reshape(local_bricks, 2, cells)
    slab = (
        gradient.reshape(NBY, NBZ, 2, E, E, E)
        .transpose(2, 3, 0, 4, 1, 5)
        .reshape(2, E, NBY * E, NBZ * E)
    )
    summed = src_sum(slab)
    padded = with_halo(summed, (("vol", 1),), 4)
    field = smooth_axis(padded, 1)
    for axis in (2, 3):
        field = smooth_axis(pad_axis(field, axis), axis)
    return field


def solution(mesh):
    in_specs = (
        P(("src", "vol"), None, None),
        P(("src", "vol")),
        P(("src", "vol")),
        P(),
        P(),
        P("src", "vol", None, None),
    )
    out_specs = P(None, "vol", None, None)
    return jax.shard_map(local, mesh=mesh, in_specs=in_specs, out_specs=out_specs, check_vma=False)
```

```python
import math

import jax
import jax.numpy as jnp
from jax import lax
from jax.experimental import pallas as pl
from jax.experimental.pallas import tpu as pltpu
from jax.sharding import PartitionSpec as P

E = 8
NFREQ = 6
NBY = 2
NBZ = 16
LANES = 128
META = 16


def with_halo(cells, sides, width):
    for axis, dim in sides:
        count = lax.axis_size(axis)
        ends = count - 1
        head = lax.slice_in_dim(cells, 0, width, axis=dim)
        tail = lax.slice_in_dim(cells, cells.shape[dim] - width, cells.shape[dim], axis=dim)
        cells = jnp.concatenate(
            [
                lax.ppermute(tail, axis, [(i, (i + 1) % count) for i in range(ends)]),
                cells,
                lax.ppermute(head, axis, [((i + 1) % count, i) for i in range(ends)]),
            ],
            axis=dim,
        )
    return cells


def tap_weights():
    raw_taps = [math.exp(-(offset - 4) * (offset - 4) / 4.5) for offset in range(9)]
    tap_total = sum(raw_taps)
    return [tap_value / tap_total for tap_value in raw_taps]


def smooth_axis(padded, axis):
    weights = tap_weights()
    length = padded.shape[axis] - 8
    summed = jnp.zeros(padded.shape[:axis] + (length,) + padded.shape[axis + 1 :], jnp.float32)
    for offset in range(9):
        summed = summed + weights[offset] * lax.slice_in_dim(
            padded, offset, offset + length, axis=axis
        )
    return summed


def pad_axis(field, axis):
    widths = [(0, 0)] * field.ndim
    widths[axis] = (4, 4)
    return jnp.pad(field, widths)


def lookup(indices, table):
    hits = indices[:, None] == jnp.arange(table.shape[0], dtype=jnp.int32)[None, :]
    return jnp.sum(jnp.where(hits, table[None, :], 0), axis=1)


def pack_kernel(src_ref, pair_ref, fwd_ref, out_ref, bricks_ref):
    dests = out_ref.shape[0]
    rows = bricks_ref.shape[1]
    group = 16
    base = pl.program_id(0) * dests * 2

    @pl.when(pl.program_id(0) == 0)
    def _():
        for start in range(0, bricks_ref.shape[0], group):
            block = jnp.swapaxes(fwd_ref[:, start : start + group, :], 0, 1)
            for j in range(group):
                bricks_ref[start + j] = block[j].reshape(rows, LANES)

    def one_dest(d, carry):
        slot = base + 2 * d
        first = src_ref[slot]
        second = src_ref[slot + 1]
        out_ref[d, 0:rows, :] = bricks_ref[jnp.maximum(first, 0)]
        out_ref[d, rows : 2 * rows, :] = bricks_ref[jnp.maximum(second, 0)]
        lane_at = lax.broadcasted_iota(jnp.int32, (META, LANES), 1)
        tags = jnp.where(lane_at == 0, pair_ref[slot], pair_ref[slot + 1])
        out_ref[d, 2 * rows : 2 * rows + META, :] = tags.astype(jnp.float32).astype(out_ref.dtype)
        return carry

    lax.fori_loop(0, dests, one_dest, 0, unroll=True)


def correlate_kernel(pair_ref, arrived_ref, adj_ref, out_ref):
    dests = arrived_ref.shape[0]
    rows = adj_ref.shape[2]
    bricks = adj_ref.shape[1]
    groups = rows // 8
    base = pl.program_id(0) * dests * 2

    def one_slot(d, s):
        k = 2 * d + s
        pair = pair_ref[base + k]
        held = jnp.maximum(pair, 0)
        fwd = arrived_ref[d, s * rows : (s + 1) * rows, :].astype(jnp.float32)
        adj = adj_ref[held // bricks, held % bricks].astype(jnp.float32)
        prod = (fwd * adj).reshape(groups, 8, LANES)
        horizontal = None
        vertical = None
        for g in range(groups):
            if g % 3 == 2:
                vertical = prod[g] if vertical is None else vertical + prod[g]
            else:
                horizontal = prod[g] if horizontal is None else horizontal + prod[g]
        out_ref[k, 0] = jnp.where(pair >= 0, horizontal, 0.0)
        out_ref[k, 1] = jnp.where(pair >= 0, vertical, 0.0)

    for d in range(dests):
        one_slot(d, 0)
        one_slot(d, 1)


def src_sum(part):
    count = lax.axis_size("src")
    me = lax.axis_index("src")
    parts = [part] + [
        lax.ppermute(part, "src", [(i, (i + k) % count) for i in range(count)])
        for k in range(1, count)
    ]
    stacked = jnp.stack(parts)
    total = lax.dynamic_index_in_dim(stacked, me % count, keepdims=False)
    for j in range(1, count):
        total = total + lax.dynamic_index_in_dim(stacked, (me - j) % count, keepdims=False)
    return total


def local(forward, item_tx, item_brick, tx_place, brick_place, adjoint):
    stored = forward.shape[0]
    channels = forward.shape[1]
    cells = forward.shape[2]
    rows = channels * cells // LANES
    src_count = lax.axis_size("src")
    vol_count = lax.axis_size("vol")
    devices = src_count * vol_count
    local_tx = adjoint.shape[0]
    local_bricks = adjoint.shape[1]
    capacity = 2
    slot_total = devices * capacity
    tx_at = lookup(item_tx, tx_place)
    brick_at = lookup(item_brick, brick_place)
    destination = tx_at // local_tx * vol_count + brick_at // local_bricks
    pair_index = tx_at % local_tx * local_bricks + brick_at % local_bricks
    positions = jnp.arange(stored, dtype=jnp.int32)
    same_owner = destination[:, None] == destination[None, :]
    earlier = positions[:, None] > positions[None, :]
    order_rank = jnp.sum((same_owner & earlier).astype(jnp.int32), axis=1)
    slot_index = destination * capacity + order_rank
    slot_hits = slot_index[None, :] == jnp.arange(slot_total, dtype=jnp.int32)[:, None]
    filled = jnp.any(slot_hits, axis=1)
    src_of_slot = jnp.where(
        filled, jnp.sum(jnp.where(slot_hits, positions[None, :], 0), axis=1), -1
    ).astype(jnp.int32)
    pair_of_slot = jnp.where(
        filled, jnp.sum(jnp.where(slot_hits, pair_index[None, :], 0), axis=1), -1
    ).astype(jnp.int32)

    chunk = 2 * rows + META
    pack_steps = 4
    correlate_steps = 2
    dests_per_step = devices // pack_steps
    payload = pl.pallas_call(
        pack_kernel,
        out_shape=jax.ShapeDtypeStruct((devices, chunk, LANES), forward.dtype),
        grid_spec=pltpu.PrefetchScalarGridSpec(
            num_scalar_prefetch=2,
            grid=(pack_steps,),
            in_specs=[pl.BlockSpec((channels, stored, cells), lambda g, s, p: (0, 0, 0))],
            out_specs=pl.BlockSpec((dests_per_step, chunk, LANES), lambda g, s, p: (g, 0, 0)),
            scratch_shapes=[pltpu.VMEM((stored, rows, LANES), forward.dtype)],
        ),
        compiler_params=pltpu.CompilerParams(vmem_limit_bytes=48 * 1024 * 1024),
    )(src_of_slot, pair_of_slot, jnp.transpose(forward, (1, 0, 2)))

    arrived = lax.all_to_all(payload, ("src", "vol"), split_axis=0, concat_axis=0, tiled=True)
    tags = arrived[:, 2 * rows, 0:2].reshape(slot_total)
    arrived_pairs = tags.astype(jnp.float32).astype(jnp.int32)

    adj_rows = jnp.transpose(
        jnp.transpose(adjoint, (0, 2, 1, 3)).reshape(local_tx, channels, local_bricks, cells // LANES, LANES),
        (0, 2, 1, 3, 4),
    ).reshape(local_tx, local_bricks, rows, LANES)
    per_slot = pl.pallas_call(
        correlate_kernel,
        out_shape=jax.ShapeDtypeStruct((slot_total, 2, 8, LANES), jnp.float32),
        grid_spec=pltpu.PrefetchScalarGridSpec(
            num_scalar_prefetch=1,
            grid=(correlate_steps,),
            in_specs=[
                pl.BlockSpec((devices // correlate_steps, chunk, LANES), lambda g, p: (g, 0, 0)),
                pl.BlockSpec((local_tx, local_bricks, rows, LANES), lambda g, p: (0, 0, 0, 0)),
            ],
            out_specs=pl.BlockSpec((2 * devices // correlate_steps, 2, 8, LANES), lambda g, p: (g, 0, 0, 0)),
        ),
        compiler_params=pltpu.CompilerParams(vmem_limit_bytes=48 * 1024 * 1024),
    )(arrived_pairs, arrived, adj_rows)

    corr = (per_slot[:, :, 0:4, :] - per_slot[:, :, 4:8, :]).reshape(slot_total, 2 * cells)
    owner_brick = jnp.maximum(arrived_pairs, 0) % local_bricks
    owner_table = (
        (owner_brick[None, :] == jnp.arange(local_bricks, dtype=jnp.int32)[:, None])
        & (arrived_pairs >= 0)[None, :]
    ).astype(jnp.float32)
    gradient = jnp.dot(owner_table, corr, precision=lax.Precision.HIGHEST).reshape(local_bricks, 2, cells)
    slab = (
        gradient.reshape(NBY, NBZ, 2, E, E, E)
        .transpose(2, 3, 0, 4, 1, 5)
        .reshape(2, E, NBY * E, NBZ * E)
    )
    summed = src_sum(slab)
    padded = with_halo(summed, (("vol", 1),), 4)
    field = smooth_axis(padded, 1)
    for axis in (2, 3):
        field = smooth_axis(pad_axis(field, axis), axis)
    return field


def solution(mesh):
    in_specs = (
        P(("src", "vol"), None, None),
        P(("src", "vol")),
        P(("src", "vol")),
        P(),
        P(),
        P("src", "vol", None, None),
    )
    out_specs = P(None, "vol", None, None)
    return jax.shard_map(local, mesh=mesh, in_specs=in_specs, out_specs=out_specs, check_vma=False)
```

```python
import math

import jax
import jax.numpy as jnp
from jax import lax
from jax.experimental import pallas as pl
from jax.experimental.pallas import tpu as pltpu
from jax.sharding import PartitionSpec as P

E = 8
NFREQ = 6
NBY = 2
NBZ = 16
LANES = 128
META = 16


def with_halo(cells, sides, width):
    for axis, dim in sides:
        count = lax.axis_size(axis)
        ends = count - 1
        head = lax.slice_in_dim(cells, 0, width, axis=dim)
        tail = lax.slice_in_dim(cells, cells.shape[dim] - width, cells.shape[dim], axis=dim)
        cells = jnp.concatenate(
            [
                lax.ppermute(tail, axis, [(i, (i + 1) % count) for i in range(ends)]),
                cells,
                lax.ppermute(head, axis, [((i + 1) % count, i) for i in range(ends)]),
            ],
            axis=dim,
        )
    return cells


def tap_weights():
    raw_taps = [math.exp(-(offset - 4) * (offset - 4) / 4.5) for offset in range(9)]
    tap_total = sum(raw_taps)
    return [tap_value / tap_total for tap_value in raw_taps]


def smooth_axis(padded, axis):
    weights = tap_weights()
    length = padded.shape[axis] - 8
    summed = jnp.zeros(padded.shape[:axis] + (length,) + padded.shape[axis + 1 :], jnp.float32)
    for offset in range(9):
        summed = summed + weights[offset] * lax.slice_in_dim(
            padded, offset, offset + length, axis=axis
        )
    return summed


def pad_axis(field, axis):
    widths = [(0, 0)] * field.ndim
    widths[axis] = (4, 4)
    return jnp.pad(field, widths)


def lookup(indices, table):
    hits = indices[:, None] == jnp.arange(table.shape[0], dtype=jnp.int32)[None, :]
    return jnp.sum(jnp.where(hits, table[None, :], 0), axis=1)


def pack_kernel(src_ref, pair_ref, fwd_ref, out_ref, bricks_ref):
    dests = out_ref.shape[0]
    rows = bricks_ref.shape[1]
    group = 16
    base = pl.program_id(0) * dests * 2

    @pl.when(pl.program_id(0) == 0)
    def _():
        for start in range(0, bricks_ref.shape[0], group):
            block = jnp.swapaxes(fwd_ref[:, start : start + group, :], 0, 1)
            for j in range(group):
                bricks_ref[start + j] = block[j].reshape(rows, LANES)

    def one_dest(d, carry):
        slot = base + 2 * d
        first = src_ref[slot]
        second = src_ref[slot + 1]
        out_ref[d, 0:rows, :] = bricks_ref[jnp.maximum(first, 0)]
        out_ref[d, rows : 2 * rows, :] = bricks_ref[jnp.maximum(second, 0)]
        lane_at = lax.broadcasted_iota(jnp.int32, (META, LANES), 1)
        tags = jnp.where(lane_at == 0, pair_ref[slot], pair_ref[slot + 1])
        out_ref[d, 2 * rows : 2 * rows + META, :] = tags.astype(jnp.float32).astype(out_ref.dtype)
        return carry

    lax.fori_loop(0, dests, one_dest, 0, unroll=True)


def correlate_kernel(pair_ref, arrived_ref, adj_ref, out_ref):
    dests = arrived_ref.shape[0]
    rows = adj_ref.shape[2]
    bricks = adj_ref.shape[1]
    groups = rows // 8
    base = pl.program_id(0) * dests * 2

    def one_slot(d, s):
        k = 2 * d + s
        pair = pair_ref[base + k]
        held = jnp.maximum(pair, 0)
        fwd = arrived_ref[d, s * rows : (s + 1) * rows, :].astype(jnp.float32)
        adj = adj_ref[held // bricks, held % bricks].astype(jnp.float32)
        prod = (fwd * adj).reshape(groups, 8, LANES)
        horizontal = None
        vertical = None
        for g in range(groups):
            if g % 3 == 2:
                vertical = prod[g] if vertical is None else vertical + prod[g]
            else:
                horizontal = prod[g] if horizontal is None else horizontal + prod[g]
        out_ref[k, 0] = jnp.where(pair >= 0, horizontal, 0.0)
        out_ref[k, 1] = jnp.where(pair >= 0, vertical, 0.0)

    for d in range(dests):
        one_slot(d, 0)
        one_slot(d, 1)


def src_sum(part):
    count = lax.axis_size("src")
    me = lax.axis_index("src")
    parts = [part] + [
        lax.ppermute(part, "src", [(i, (i + k) % count) for i in range(count)])
        for k in range(1, count)
    ]
    stacked = jnp.stack(parts)
    total = lax.dynamic_index_in_dim(stacked, me % count, keepdims=False)
    for j in range(1, count):
        total = total + lax.dynamic_index_in_dim(stacked, (me - j) % count, keepdims=False)
    return total


def local(forward, item_tx, item_brick, tx_place, brick_place, adjoint):
    stored = forward.shape[0]
    channels = forward.shape[1]
    cells = forward.shape[2]
    rows = channels * cells // LANES
    src_count = lax.axis_size("src")
    vol_count = lax.axis_size("vol")
    devices = src_count * vol_count
    local_tx = adjoint.shape[0]
    local_bricks = adjoint.shape[1]
    capacity = 2
    slot_total = devices * capacity
    tx_at = lookup(item_tx, tx_place)
    brick_at = lookup(item_brick, brick_place)
    destination = tx_at // local_tx * vol_count + brick_at // local_bricks
    pair_index = tx_at % local_tx * local_bricks + brick_at % local_bricks
    positions = jnp.arange(stored, dtype=jnp.int32)
    same_owner = destination[:, None] == destination[None, :]
    earlier = positions[:, None] > positions[None, :]
    order_rank = jnp.sum((same_owner & earlier).astype(jnp.int32), axis=1)
    slot_index = destination * capacity + order_rank
    slot_hits = slot_index[None, :] == jnp.arange(slot_total, dtype=jnp.int32)[:, None]
    filled = jnp.any(slot_hits, axis=1)
    src_of_slot = jnp.where(
        filled, jnp.sum(jnp.where(slot_hits, positions[None, :], 0), axis=1), -1
    ).astype(jnp.int32)
    pair_of_slot = jnp.where(
        filled, jnp.sum(jnp.where(slot_hits, pair_index[None, :], 0), axis=1), -1
    ).astype(jnp.int32)

    chunk = 2 * rows + META
    pack_steps = 2
    correlate_steps = 2
    dests_per_step = devices // pack_steps
    payload = pl.pallas_call(
        pack_kernel,
        out_shape=jax.ShapeDtypeStruct((devices, chunk, LANES), forward.dtype),
        grid_spec=pltpu.PrefetchScalarGridSpec(
            num_scalar_prefetch=2,
            grid=(pack_steps,),
            in_specs=[pl.BlockSpec((channels, stored, cells), lambda g, s, p: (0, 0, 0))],
            out_specs=pl.BlockSpec((dests_per_step, chunk, LANES), lambda g, s, p: (g, 0, 0)),
            scratch_shapes=[pltpu.VMEM((stored, rows, LANES), forward.dtype)],
        ),
        compiler_params=pltpu.CompilerParams(vmem_limit_bytes=48 * 1024 * 1024),
    )(src_of_slot, pair_of_slot, jnp.transpose(forward, (1, 0, 2)))

    arrived = lax.all_to_all(payload, ("src", "vol"), split_axis=0, concat_axis=0, tiled=True)
    tags = arrived[:, 2 * rows, 0:2].reshape(slot_total)
    arrived_pairs = tags.astype(jnp.float32).astype(jnp.int32)

    adj_rows = jnp.transpose(
        jnp.transpose(adjoint, (0, 2, 1, 3)).reshape(local_tx, channels, local_bricks, cells // LANES, LANES),
        (0, 2, 1, 3, 4),
    ).reshape(local_tx, local_bricks, rows, LANES)
    per_slot = pl.pallas_call(
        correlate_kernel,
        out_shape=jax.ShapeDtypeStruct((slot_total, 2, 8, LANES), jnp.float32),
        grid_spec=pltpu.PrefetchScalarGridSpec(
            num_scalar_prefetch=1,
            grid=(correlate_steps,),
            in_specs=[
                pl.BlockSpec((devices // correlate_steps, chunk, LANES), lambda g, p: (g, 0, 0)),
                pl.BlockSpec((local_tx, local_bricks, rows, LANES), lambda g, p: (0, 0, 0, 0)),
            ],
            out_specs=pl.BlockSpec((2 * devices // correlate_steps, 2, 8, LANES), lambda g, p: (g, 0, 0, 0)),
        ),
        compiler_params=pltpu.CompilerParams(vmem_limit_bytes=48 * 1024 * 1024),
    )(arrived_pairs, arrived, adj_rows)

    corr = (per_slot[:, :, 0:4, :] - per_slot[:, :, 4:8, :]).reshape(slot_total, 2 * cells)
    owner_brick = jnp.maximum(arrived_pairs, 0) % local_bricks
    owner_table = (
        (owner_brick[None, :] == jnp.arange(local_bricks, dtype=jnp.int32)[:, None])
        & (arrived_pairs >= 0)[None, :]
    ).astype(jnp.float32)
    gradient = jnp.dot(owner_table, corr, precision=lax.Precision.HIGHEST).reshape(local_bricks, 2, cells)
    slab = (
        gradient.reshape(NBY, NBZ, 2, E, E, E)
        .transpose(2, 3, 0, 4, 1, 5)
        .reshape(2, E, NBY * E, NBZ * E)
    )
    summed = src_sum(slab)
    padded = with_halo(summed, (("vol", 1),), 4)
    field = smooth_axis(padded, 1)
    for axis in (2, 3):
        field = smooth_axis(pad_axis(field, axis), axis)
    return field


def solution(mesh):
    in_specs = (
        P(("src", "vol"), None, None),
        P(("src", "vol")),
        P(("src", "vol")),
        P(),
        P(),
        P("src", "vol", None, None),
    )
    out_specs = P(None, "vol", None, None)
    return jax.shard_map(local, mesh=mesh, in_specs=in_specs, out_specs=out_specs, check_vma=False)
```

```python
import math

import jax
import jax.numpy as jnp
from jax import lax
from jax.experimental import pallas as pl
from jax.experimental.pallas import tpu as pltpu
from jax.sharding import PartitionSpec as P

E = 8
NFREQ = 6
NBY = 2
NBZ = 16
LANES = 128
META = 16


def with_halo(cells, sides, width):
    for axis, dim in sides:
        count = lax.axis_size(axis)
        ends = count - 1
        head = lax.slice_in_dim(cells, 0, width, axis=dim)
        tail = lax.slice_in_dim(cells, cells.shape[dim] - width, cells.shape[dim], axis=dim)
        cells = jnp.concatenate(
            [
                lax.ppermute(tail, axis, [(i, (i + 1) % count) for i in range(ends)]),
                cells,
                lax.ppermute(head, axis, [((i + 1) % count, i) for i in range(ends)]),
            ],
            axis=dim,
        )
    return cells


def tap_weights():
    raw_taps = [math.exp(-(offset - 4) * (offset - 4) / 4.5) for offset in range(9)]
    tap_total = sum(raw_taps)
    return [tap_value / tap_total for tap_value in raw_taps]


def smooth_axis(padded, axis):
    weights = tap_weights()
    length = padded.shape[axis] - 8
    summed = jnp.zeros(padded.shape[:axis] + (length,) + padded.shape[axis + 1 :], jnp.float32)
    for offset in range(9):
        summed = summed + weights[offset] * lax.slice_in_dim(
            padded, offset, offset + length, axis=axis
        )
    return summed


def pad_axis(field, axis):
    widths = [(0, 0)] * field.ndim
    widths[axis] = (4, 4)
    return jnp.pad(field, widths)


def pack_kernel(src_ref, pair_ref, fwd_ref, out_ref, bricks_ref):
    dests = out_ref.shape[0]
    rows = bricks_ref.shape[1]
    group = 16
    base = pl.program_id(0) * dests * 2

    @pl.when(pl.program_id(0) == 0)
    def _():
        for start in range(0, bricks_ref.shape[0], group):
            block = jnp.swapaxes(fwd_ref[:, start : start + group, :], 0, 1)
            for j in range(group):
                bricks_ref[start + j] = block[j].reshape(rows, LANES)

    def one_dest(d, carry):
        slot = base + 2 * d
        first = src_ref[slot]
        second = src_ref[slot + 1]
        out_ref[d, 0:rows, :] = bricks_ref[jnp.maximum(first, 0)]
        out_ref[d, rows : 2 * rows, :] = bricks_ref[jnp.maximum(second, 0)]
        lane_at = lax.broadcasted_iota(jnp.int32, (META, LANES), 1)
        tags = jnp.where(lane_at == 0, pair_ref[slot], pair_ref[slot + 1])
        out_ref[d, 2 * rows : 2 * rows + META, :] = tags.astype(jnp.float32).astype(out_ref.dtype)
        return carry

    lax.fori_loop(0, dests, one_dest, 0, unroll=True)


def correlate_kernel(pair_ref, arrived_ref, adj_ref, out_ref):
    dests = arrived_ref.shape[0]
    rows = adj_ref.shape[2]
    bricks = adj_ref.shape[1]
    groups = rows // 8
    base = pl.program_id(0) * dests * 2

    def one_slot(d, s):
        k = 2 * d + s
        pair = pair_ref[base + k]
        held = jnp.maximum(pair, 0)
        fwd = arrived_ref[d, s * rows : (s + 1) * rows, :].astype(jnp.float32)
        adj = adj_ref[held // bricks, held % bricks].astype(jnp.float32)
        prod = (fwd * adj).reshape(groups, 8, LANES)
        horizontal = None
        vertical = None
        for g in range(groups):
            if g % 3 == 2:
                vertical = prod[g] if vertical is None else vertical + prod[g]
            else:
                horizontal = prod[g] if horizontal is None else horizontal + prod[g]
        out_ref[k, 0] = jnp.where(pair >= 0, horizontal, 0.0)
        out_ref[k, 1] = jnp.where(pair >= 0, vertical, 0.0)

    for d in range(dests):
        one_slot(d, 0)
        one_slot(d, 1)


def src_sum(part):
    count = lax.axis_size("src")
    me = lax.axis_index("src")
    parts = [part] + [
        lax.ppermute(part, "src", [(i, (i + k) % count) for i in range(count)])
        for k in range(1, count)
    ]
    stacked = jnp.stack(parts)
    total = lax.dynamic_index_in_dim(stacked, me % count, keepdims=False)
    for j in range(1, count):
        total = total + lax.dynamic_index_in_dim(stacked, (me - j) % count, keepdims=False)
    return total


def local(forward, item_tx, item_brick, tx_place, brick_place, adjoint):
    stored = forward.shape[0]
    channels = forward.shape[1]
    cells = forward.shape[2]
    rows = channels * cells // LANES
    src_count = lax.axis_size("src")
    vol_count = lax.axis_size("vol")
    devices = src_count * vol_count
    local_tx = adjoint.shape[0]
    local_bricks = adjoint.shape[1]
    capacity = 2
    slot_total = devices * capacity
    tx_at = jnp.take(tx_place, item_tx, mode="clip")
    brick_at = jnp.take(brick_place, item_brick, mode="clip")
    destination = tx_at // local_tx * vol_count + brick_at // local_bricks
    pair_index = tx_at % local_tx * local_bricks + brick_at % local_bricks
    positions = jnp.arange(stored, dtype=jnp.int32)
    same_owner = destination[:, None] == destination[None, :]
    earlier = positions[:, None] > positions[None, :]
    order_rank = jnp.sum((same_owner & earlier).astype(jnp.int32), axis=1)
    slot_index = destination * capacity + order_rank
    slot_hits = slot_index[None, :] == jnp.arange(slot_total, dtype=jnp.int32)[:, None]
    filled = jnp.any(slot_hits, axis=1)
    src_of_slot = jnp.where(
        filled, jnp.sum(jnp.where(slot_hits, positions[None, :], 0), axis=1), -1
    ).astype(jnp.int32)
    pair_of_slot = jnp.where(
        filled, jnp.sum(jnp.where(slot_hits, pair_index[None, :], 0), axis=1), -1
    ).astype(jnp.int32)

    chunk = 2 * rows + META
    pack_steps = 2
    correlate_steps = 2
    dests_per_step = devices // pack_steps
    payload = pl.pallas_call(
        pack_kernel,
        out_shape=jax.ShapeDtypeStruct((devices, chunk, LANES), forward.dtype),
        grid_spec=pltpu.PrefetchScalarGridSpec(
            num_scalar_prefetch=2,
            grid=(pack_steps,),
            in_specs=[pl.BlockSpec((channels, stored, cells), lambda g, s, p: (0, 0, 0))],
            out_specs=pl.BlockSpec((dests_per_step, chunk, LANES), lambda g, s, p: (g, 0, 0)),
            scratch_shapes=[pltpu.VMEM((stored, rows, LANES), forward.dtype)],
        ),
        compiler_params=pltpu.CompilerParams(vmem_limit_bytes=48 * 1024 * 1024),
    )(src_of_slot, pair_of_slot, jnp.transpose(forward, (1, 0, 2)))

    arrived = lax.all_to_all(payload, ("src", "vol"), split_axis=0, concat_axis=0, tiled=True)
    tags = arrived[:, 2 * rows, 0:2].reshape(slot_total)
    arrived_pairs = tags.astype(jnp.float32).astype(jnp.int32)

    adj_rows = jnp.transpose(
        jnp.transpose(adjoint, (0, 2, 1, 3)).reshape(local_tx, channels, local_bricks, cells // LANES, LANES),
        (0, 2, 1, 3, 4),
    ).reshape(local_tx, local_bricks, rows, LANES)
    per_slot = pl.pallas_call(
        correlate_kernel,
        out_shape=jax.ShapeDtypeStruct((slot_total, 2, 8, LANES), jnp.float32),
        grid_spec=pltpu.PrefetchScalarGridSpec(
            num_scalar_prefetch=1,
            grid=(correlate_steps,),
            in_specs=[
                pl.BlockSpec((devices // correlate_steps, chunk, LANES), lambda g, p: (g, 0, 0)),
                pl.BlockSpec((local_tx, local_bricks, rows, LANES), lambda g, p: (0, 0, 0, 0)),
            ],
            out_specs=pl.BlockSpec((2 * devices // correlate_steps, 2, 8, LANES), lambda g, p: (g, 0, 0, 0)),
        ),
        compiler_params=pltpu.CompilerParams(vmem_limit_bytes=48 * 1024 * 1024),
    )(arrived_pairs, arrived, adj_rows)

    corr = (per_slot[:, :, 0:4, :] - per_slot[:, :, 4:8, :]).reshape(slot_total, 2 * cells)
    owner_brick = jnp.maximum(arrived_pairs, 0) % local_bricks
    owner_table = (
        (owner_brick[None, :] == jnp.arange(local_bricks, dtype=jnp.int32)[:, None])
        & (arrived_pairs >= 0)[None, :]
    ).astype(jnp.float32)
    gradient = jnp.dot(owner_table, corr, precision=lax.Precision.HIGHEST).reshape(local_bricks, 2, cells)
    slab = (
        gradient.reshape(NBY, NBZ, 2, E, E, E)
        .transpose(2, 3, 0, 4, 1, 5)
        .reshape(2, E, NBY * E, NBZ * E)
    )
    summed = src_sum(slab)
    padded = with_halo(summed, (("vol", 1),), 4)
    field = smooth_axis(padded, 1)
    for axis in (2, 3):
        field = smooth_axis(pad_axis(field, axis), axis)
    return field


def solution(mesh):
    in_specs = (
        P(("src", "vol"), None, None),
        P(("src", "vol")),
        P(("src", "vol")),
        P(),
        P(),
        P("src", "vol", None, None),
    )
    out_specs = P(None, "vol", None, None)
    return jax.shard_map(local, mesh=mesh, in_specs=in_specs, out_specs=out_specs, check_vma=False)
```

```python
import math

import jax
import jax.numpy as jnp
from jax import lax
from jax.experimental import pallas as pl
from jax.experimental.pallas import tpu as pltpu
from jax.sharding import PartitionSpec as P

E = 8
NFREQ = 6
NBY = 2
NBZ = 16
LANES = 128
META = 16


def with_halo(cells, sides, width):
    for axis, dim in sides:
        count = lax.axis_size(axis)
        ends = count - 1
        head = lax.slice_in_dim(cells, 0, width, axis=dim)
        tail = lax.slice_in_dim(cells, cells.shape[dim] - width, cells.shape[dim], axis=dim)
        cells = jnp.concatenate(
            [
                lax.ppermute(tail, axis, [(i, (i + 1) % count) for i in range(ends)]),
                cells,
                lax.ppermute(head, axis, [((i + 1) % count, i) for i in range(ends)]),
            ],
            axis=dim,
        )
    return cells


def tap_weights():
    raw_taps = [math.exp(-(offset - 4) * (offset - 4) / 4.5) for offset in range(9)]
    tap_total = sum(raw_taps)
    return [tap_value / tap_total for tap_value in raw_taps]


def smooth_axis(padded, axis):
    weights = tap_weights()
    length = padded.shape[axis] - 8
    summed = jnp.zeros(padded.shape[:axis] + (length,) + padded.shape[axis + 1 :], jnp.float32)
    for offset in range(9):
        summed = summed + weights[offset] * lax.slice_in_dim(
            padded, offset, offset + length, axis=axis
        )
    return summed


def pad_axis(field, axis):
    widths = [(0, 0)] * field.ndim
    widths[axis] = (4, 4)
    return jnp.pad(field, widths)


def lookup(indices, table):
    hits = indices[:, None] == jnp.arange(table.shape[0], dtype=jnp.int32)[None, :]
    return jnp.sum(jnp.where(hits, table[None, :], 0), axis=1)


def pack_kernel(src_ref, pair_ref, fwd_ref, out_ref, bricks_ref):
    dests = out_ref.shape[0]
    rows = bricks_ref.shape[1]
    group = 16
    base = pl.program_id(0) * dests * 2

    @pl.when(pl.program_id(0) == 0)
    def _():
        for start in range(0, bricks_ref.shape[0], group):
            block = jnp.swapaxes(fwd_ref[:, start : start + group, :], 0, 1)
            for j in range(group):
                bricks_ref[start + j] = block[j].reshape(rows, LANES)

    def one_dest(d, carry):
        slot = base + 2 * d
        first = src_ref[slot]
        second = src_ref[slot + 1]
        out_ref[d, 0:rows, :] = bricks_ref[jnp.maximum(first, 0)]
        out_ref[d, rows : 2 * rows, :] = bricks_ref[jnp.maximum(second, 0)]
        lane_at = lax.broadcasted_iota(jnp.int32, (META, LANES), 1)
        tags = jnp.where(lane_at == 0, pair_ref[slot], pair_ref[slot + 1])
        out_ref[d, 2 * rows : 2 * rows + META, :] = tags.astype(jnp.float32).astype(out_ref.dtype)
        return carry

    lax.fori_loop(0, dests, one_dest, 0, unroll=True)


def correlate_kernel(pair_ref, arrived_ref, adj_ref, out_ref):
    dests = arrived_ref.shape[0]
    rows = adj_ref.shape[2]
    bricks = adj_ref.shape[1]
    groups = rows // 8
    base = pl.program_id(0) * dests * 2

    def one_slot(d, s):
        k = 2 * d + s
        pair = pair_ref[base + k]
        held = jnp.maximum(pair, 0)
        fwd = arrived_ref[d, s * rows : (s + 1) * rows, :].astype(jnp.float32)
        adj = adj_ref[held // bricks, held % bricks].astype(jnp.float32)
        prod = (fwd * adj).reshape(groups, 8, LANES)
        horizontal = None
        vertical = None
        for g in range(groups):
            if g % 3 == 2:
                vertical = prod[g] if vertical is None else vertical + prod[g]
            else:
                horizontal = prod[g] if horizontal is None else horizontal + prod[g]
        out_ref[k, 0] = jnp.where(pair >= 0, horizontal, 0.0)
        out_ref[k, 1] = jnp.where(pair >= 0, vertical, 0.0)

    for d in range(dests):
        one_slot(d, 0)
        one_slot(d, 1)


def src_sum(part):
    count = lax.axis_size("src")
    me = lax.axis_index("src")
    parts = [part] + [
        lax.ppermute(part, "src", [(i, (i + k) % count) for i in range(count)])
        for k in range(1, count)
    ]
    stacked = jnp.stack(parts)
    total = lax.dynamic_index_in_dim(stacked, me % count, keepdims=False)
    for j in range(1, count):
        total = total + lax.dynamic_index_in_dim(stacked, (me - j) % count, keepdims=False)
    return total


def local(forward, item_tx, item_brick, tx_place, brick_place, adjoint):
    stored = forward.shape[0]
    channels = forward.shape[1]
    cells = forward.shape[2]
    rows = channels * cells // LANES
    src_count = lax.axis_size("src")
    vol_count = lax.axis_size("vol")
    devices = src_count * vol_count
    local_tx = adjoint.shape[0]
    local_bricks = adjoint.shape[1]
    capacity = 2
    slot_total = devices * capacity
    tx_at = lookup(item_tx, tx_place)
    brick_at = lookup(item_brick, brick_place)
    destination = tx_at // local_tx * vol_count + brick_at // local_bricks
    pair_index = tx_at % local_tx * local_bricks + brick_at % local_bricks
    positions = jnp.arange(stored, dtype=jnp.int32)
    same_owner = destination[:, None] == destination[None, :]
    earlier = positions[:, None] > positions[None, :]
    order_rank = jnp.sum((same_owner & earlier).astype(jnp.int32), axis=1)
    slot_index = destination * capacity + order_rank
    slot_hits = slot_index[None, :] == jnp.arange(slot_total, dtype=jnp.int32)[:, None]
    filled = jnp.any(slot_hits, axis=1)
    src_of_slot = jnp.where(
        filled, jnp.sum(jnp.where(slot_hits, positions[None, :], 0), axis=1), -1
    ).astype(jnp.int32)
    pair_of_slot = jnp.where(
        filled, jnp.sum(jnp.where(slot_hits, pair_index[None, :], 0), axis=1), -1
    ).astype(jnp.int32)

    chunk = 2 * rows + META
    pack_steps = 2
    correlate_steps = 1
    dests_per_step = devices // pack_steps
    payload = pl.pallas_call(
        pack_kernel,
        out_shape=jax.ShapeDtypeStruct((devices, chunk, LANES), forward.dtype),
        grid_spec=pltpu.PrefetchScalarGridSpec(
            num_scalar_prefetch=2,
            grid=(pack_steps,),
            in_specs=[pl.BlockSpec((channels, stored, cells), lambda g, s, p: (0, 0, 0))],
            out_specs=pl.BlockSpec((dests_per_step, chunk, LANES), lambda g, s, p: (g, 0, 0)),
            scratch_shapes=[pltpu.VMEM((stored, rows, LANES), forward.dtype)],
        ),
        compiler_params=pltpu.CompilerParams(vmem_limit_bytes=48 * 1024 * 1024),
    )(src_of_slot, pair_of_slot, jnp.transpose(forward, (1, 0, 2)))

    arrived = lax.all_to_all(payload, ("src", "vol"), split_axis=0, concat_axis=0, tiled=True)
    tags = arrived[:, 2 * rows, 0:2].reshape(slot_total)
    arrived_pairs = tags.astype(jnp.float32).astype(jnp.int32)

    adj_rows = jnp.transpose(
        jnp.transpose(adjoint, (0, 2, 1, 3)).reshape(local_tx, channels, local_bricks, cells // LANES, LANES),
        (0, 2, 1, 3, 4),
    ).reshape(local_tx, local_bricks, rows, LANES)
    per_slot = pl.pallas_call(
        correlate_kernel,
        out_shape=jax.ShapeDtypeStruct((slot_total, 2, 8, LANES), jnp.float32),
        grid_spec=pltpu.PrefetchScalarGridSpec(
            num_scalar_prefetch=1,
            grid=(correlate_steps,),
            in_specs=[
                pl.BlockSpec((devices // correlate_steps, chunk, LANES), lambda g, p: (g, 0, 0)),
                pl.BlockSpec((local_tx, local_bricks, rows, LANES), lambda g, p: (0, 0, 0, 0)),
            ],
            out_specs=pl.BlockSpec((2 * devices // correlate_steps, 2, 8, LANES), lambda g, p: (g, 0, 0, 0)),
        ),
        compiler_params=pltpu.CompilerParams(vmem_limit_bytes=48 * 1024 * 1024),
    )(arrived_pairs, arrived, adj_rows)

    corr = (per_slot[:, :, 0:4, :] - per_slot[:, :, 4:8, :]).reshape(slot_total, 2 * cells)
    owner_brick = jnp.maximum(arrived_pairs, 0) % local_bricks
    owner_table = (
        (owner_brick[None, :] == jnp.arange(local_bricks, dtype=jnp.int32)[:, None])
        & (arrived_pairs >= 0)[None, :]
    ).astype(jnp.float32)
    gradient = jnp.dot(owner_table, corr, precision=lax.Precision.HIGHEST).reshape(local_bricks, 2, cells)
    slab = (
        gradient.reshape(NBY, NBZ, 2, E, E, E)
        .transpose(2, 3, 0, 4, 1, 5)
        .reshape(2, E, NBY * E, NBZ * E)
    )
    summed = src_sum(slab)
    padded = with_halo(summed, (("vol", 1),), 4)
    field = smooth_axis(padded, 1)
    for axis in (2, 3):
        field = smooth_axis(pad_axis(field, axis), axis)
    return field


def solution(mesh):
    in_specs = (
        P(("src", "vol"), None, None),
        P(("src", "vol")),
        P(("src", "vol")),
        P(),
        P(),
        P("src", "vol", None, None),
    )
    out_specs = P(None, "vol", None, None)
    return jax.shard_map(local, mesh=mesh, in_specs=in_specs, out_specs=out_specs, check_vma=False)
```

```python
import math

import jax
import jax.numpy as jnp
from jax import lax
from jax.experimental import pallas as pl
from jax.experimental.pallas import tpu as pltpu
from jax.sharding import PartitionSpec as P

E = 8
NFREQ = 6
NBY = 2
NBZ = 16
LANES = 128
META = 16


def with_halo(cells, sides, width):
    for axis, dim in sides:
        count = lax.axis_size(axis)
        ends = count - 1
        head = lax.slice_in_dim(cells, 0, width, axis=dim)
        tail = lax.slice_in_dim(cells, cells.shape[dim] - width, cells.shape[dim], axis=dim)
        cells = jnp.concatenate(
            [
                lax.ppermute(tail, axis, [(i, (i + 1) % count) for i in range(ends)]),
                cells,
                lax.ppermute(head, axis, [((i + 1) % count, i) for i in range(ends)]),
            ],
            axis=dim,
        )
    return cells


def tap_weights():
    raw_taps = [math.exp(-(offset - 4) * (offset - 4) / 4.5) for offset in range(9)]
    tap_total = sum(raw_taps)
    return [tap_value / tap_total for tap_value in raw_taps]


def smooth_axis(padded, axis):
    weights = tap_weights()
    length = padded.shape[axis] - 8
    summed = jnp.zeros(padded.shape[:axis] + (length,) + padded.shape[axis + 1 :], jnp.float32)
    for offset in range(9):
        summed = summed + weights[offset] * lax.slice_in_dim(
            padded, offset, offset + length, axis=axis
        )
    return summed


def pad_axis(field, axis):
    widths = [(0, 0)] * field.ndim
    widths[axis] = (4, 4)
    return jnp.pad(field, widths)


def lookup(indices, table):
    hits = indices[:, None] == jnp.arange(table.shape[0], dtype=jnp.int32)[None, :]
    return jnp.sum(jnp.where(hits, table[None, :], 0), axis=1)


def pack_kernel(src_ref, pair_ref, fwd_ref, out_ref, bricks_ref):
    dests = out_ref.shape[0]
    rows = bricks_ref.shape[1]
    group = 16
    base = pl.program_id(0) * dests * 2

    @pl.when(pl.program_id(0) == 0)
    def _():
        for start in range(0, bricks_ref.shape[0], group):
            block = jnp.swapaxes(fwd_ref[:, start : start + group, :], 0, 1)
            for j in range(group):
                bricks_ref[start + j] = block[j].reshape(rows, LANES)

    def one_dest(d, carry):
        slot = base + 2 * d
        first = src_ref[slot]
        second = src_ref[slot + 1]
        out_ref[d, 0:rows, :] = bricks_ref[jnp.maximum(first, 0)]
        out_ref[d, rows : 2 * rows, :] = bricks_ref[jnp.maximum(second, 0)]
        lane_at = lax.broadcasted_iota(jnp.int32, (META, LANES), 1)
        tags = jnp.where(lane_at == 0, pair_ref[slot], pair_ref[slot + 1])
        out_ref[d, 2 * rows : 2 * rows + META, :] = tags.astype(jnp.float32).astype(out_ref.dtype)
        return carry

    lax.fori_loop(0, dests, one_dest, 0, unroll=True)


def correlate_kernel(pair_ref, arrived_ref, adj_ref, out_ref):
    dests = arrived_ref.shape[0]
    rows = adj_ref.shape[2]
    bricks = adj_ref.shape[1]
    groups = rows // 8
    base = pl.program_id(0) * dests * 2

    def one_slot(d, s):
        k = 2 * d + s
        pair = pair_ref[base + k]
        held = jnp.maximum(pair, 0)
        fwd = arrived_ref[d, s * rows : (s + 1) * rows, :].astype(jnp.float32)
        adj = adj_ref[held // bricks, held % bricks].astype(jnp.float32)
        prod = (fwd * adj).reshape(groups, 8, LANES)
        horizontal = None
        vertical = None
        for g in range(groups):
            if g % 3 == 2:
                vertical = prod[g] if vertical is None else vertical + prod[g]
            else:
                horizontal = prod[g] if horizontal is None else horizontal + prod[g]
        out_ref[k, 0] = jnp.where(pair >= 0, horizontal, 0.0)
        out_ref[k, 1] = jnp.where(pair >= 0, vertical, 0.0)

    for d in range(dests):
        one_slot(d, 0)
        one_slot(d, 1)


def src_sum(part):
    count = lax.axis_size("src")
    me = lax.axis_index("src")
    parts = [part] + [
        lax.ppermute(part, "src", [(i, (i + k) % count) for i in range(count)])
        for k in range(1, count)
    ]

    def from_src(j):
        shift = (me - j) % count
        picked = parts[0]
        for k in range(1, count):
            picked = jnp.where(shift == k, parts[k], picked)
        return picked

    total = from_src(0)
    for j in range(1, count):
        total = total + from_src(j)
    return total


def local(forward, item_tx, item_brick, tx_place, brick_place, adjoint):
    stored = forward.shape[0]
    channels = forward.shape[1]
    cells = forward.shape[2]
    rows = channels * cells // LANES
    src_count = lax.axis_size("src")
    vol_count = lax.axis_size("vol")
    devices = src_count * vol_count
    local_tx = adjoint.shape[0]
    local_bricks = adjoint.shape[1]
    capacity = 2
    slot_total = devices * capacity
    tx_at = lookup(item_tx, tx_place)
    brick_at = lookup(item_brick, brick_place)
    destination = tx_at // local_tx * vol_count + brick_at // local_bricks
    pair_index = tx_at % local_tx * local_bricks + brick_at % local_bricks
    positions = jnp.arange(stored, dtype=jnp.int32)
    same_owner = destination[:, None] == destination[None, :]
    earlier = positions[:, None] > positions[None, :]
    order_rank = jnp.sum((same_owner & earlier).astype(jnp.int32), axis=1)
    slot_index = destination * capacity + order_rank
    slot_hits = slot_index[None, :] == jnp.arange(slot_total, dtype=jnp.int32)[:, None]
    filled = jnp.any(slot_hits, axis=1)
    src_of_slot = jnp.where(
        filled, jnp.sum(jnp.where(slot_hits, positions[None, :], 0), axis=1), -1
    ).astype(jnp.int32)
    pair_of_slot = jnp.where(
        filled, jnp.sum(jnp.where(slot_hits, pair_index[None, :], 0), axis=1), -1
    ).astype(jnp.int32)

    chunk = 2 * rows + META
    pack_steps = 2
    correlate_steps = 2
    dests_per_step = devices // pack_steps
    payload = pl.pallas_call(
        pack_kernel,
        out_shape=jax.ShapeDtypeStruct((devices, chunk, LANES), forward.dtype),
        grid_spec=pltpu.PrefetchScalarGridSpec(
            num_scalar_prefetch=2,
            grid=(pack_steps,),
            in_specs=[pl.BlockSpec((channels, stored, cells), lambda g, s, p: (0, 0, 0))],
            out_specs=pl.BlockSpec((dests_per_step, chunk, LANES), lambda g, s, p: (g, 0, 0)),
            scratch_shapes=[pltpu.VMEM((stored, rows, LANES), forward.dtype)],
        ),
        compiler_params=pltpu.CompilerParams(vmem_limit_bytes=48 * 1024 * 1024),
    )(src_of_slot, pair_of_slot, jnp.transpose(forward, (1, 0, 2)))

    arrived = lax.all_to_all(payload, ("src", "vol"), split_axis=0, concat_axis=0, tiled=True)
    tags = arrived[:, 2 * rows, 0:2].reshape(slot_total)
    arrived_pairs = tags.astype(jnp.float32).astype(jnp.int32)

    adj_rows = jnp.transpose(
        jnp.transpose(adjoint, (0, 2, 1, 3)).reshape(local_tx, channels, local_bricks, cells // LANES, LANES),
        (0, 2, 1, 3, 4),
    ).reshape(local_tx, local_bricks, rows, LANES)
    per_slot = pl.pallas_call(
        correlate_kernel,
        out_shape=jax.ShapeDtypeStruct((slot_total, 2, 8, LANES), jnp.float32),
        grid_spec=pltpu.PrefetchScalarGridSpec(
            num_scalar_prefetch=1,
            grid=(correlate_steps,),
            in_specs=[
                pl.BlockSpec((devices // correlate_steps, chunk, LANES), lambda g, p: (g, 0, 0)),
                pl.BlockSpec((local_tx, local_bricks, rows, LANES), lambda g, p: (0, 0, 0, 0)),
            ],
            out_specs=pl.BlockSpec((2 * devices // correlate_steps, 2, 8, LANES), lambda g, p: (g, 0, 0, 0)),
        ),
        compiler_params=pltpu.CompilerParams(vmem_limit_bytes=48 * 1024 * 1024),
    )(arrived_pairs, arrived, adj_rows)

    corr = (per_slot[:, :, 0:4, :] - per_slot[:, :, 4:8, :]).reshape(slot_total, 2 * cells)
    owner_brick = jnp.maximum(arrived_pairs, 0) % local_bricks
    owner_table = (
        (owner_brick[None, :] == jnp.arange(local_bricks, dtype=jnp.int32)[:, None])
        & (arrived_pairs >= 0)[None, :]
    ).astype(jnp.float32)
    gradient = jnp.dot(owner_table, corr, precision=lax.Precision.HIGHEST).reshape(local_bricks, 2, cells)
    slab = (
        gradient.reshape(NBY, NBZ, 2, E, E, E)
        .transpose(2, 3, 0, 4, 1, 5)
        .reshape(2, E, NBY * E, NBZ * E)
    )
    summed = src_sum(slab)
    padded = with_halo(summed, (("vol", 1),), 4)
    field = smooth_axis(padded, 1)
    for axis in (2, 3):
        field = smooth_axis(pad_axis(field, axis), axis)
    return field


def solution(mesh):
    in_specs = (
        P(("src", "vol"), None, None),
        P(("src", "vol")),
        P(("src", "vol")),
        P(),
        P(),
        P("src", "vol", None, None),
    )
    out_specs = P(None, "vol", None, None)
    return jax.shard_map(local, mesh=mesh, in_specs=in_specs, out_specs=out_specs, check_vma=False)
```
